128 devices in a mesh: half: 2 (over core), row: 8 (over z_hi, x), col: 8 (over y, z_lo).
Axes of the slice: x: 4, y: 4, z: 4 (z_hi: 2, z_lo: 2; z = z_hi * 2 + z_lo), core: 2. Of those that a mesh axis runs over, the one named last changes fastest.
Arguments:
- child_diag: float32 [2, 512, 512], P('half'), as said below
- child_panel: float32 [2, 16, 8, 128, 512], P('half', None, 'row'), may hold values from -18 to 18
- child_window: float32 [2, 16, 8, 128, 8, 8, 128], P('half', None, 'row', None, None, 'col'), may hold values from -6 to 6
- parent_diag: float32 [512, 512], replicated
- parent_lead_panel: float32 [24, 8, 2, 8, 8, 512], P(None, 'row', 'half', 'col'), may hold values from -24 to 24
- index_maps: int32 [2, 128], replicated, may hold values from 0 to 191, as said below
Outputs:
- parent_front: float32 [24, 8, 128, 4, 2, 8, 128], P(None, 'row', None, None, 'half', 'col')
- parent_factor: float32 [24, 8, 2, 8, 8, 512], P(None, 'row', 'half', 'col')
- parent_pivot: float32 [512, 512], replicated
The draws below stay inside these ranges and needn't reach their ends.
Inputs may be any that keep to these rules, and one draw needn't show every extreme that they name: child_diag and parent_diag are symmetric and positive definite. For each child k and each group a, the entries index_maps[k, a * 16 + u] with 0 <= u < 16 equal q * 16 + ((u + s) mod 16) for a group target q and a turn s fixed within the group; groups a < 4 have q = a, later groups have distinct q that rise with a; over the 8 groups of a child the turns s, taken modulo 8, are all different; for each child some group a < 4 has a turn divisible by 8, and another group a < 4 has a turn that leaves 1 modulo 8.
All inputs are finite; a program needn't handle non-finite values.
Results may differ from the reference program's by a relative error of at most 0.0001.
Values sent between devices are 32-bit elements; how exact they have to be, the bound alone decides.
No kernel may reach another device: no remote copies, remote signals or barrier semaphores. Data moves between devices by JAX's collectives and lax.ppermute only.
A program may use at most 192 MiB of HBM per device.

```python
import jax
import jax.numpy as jnp
from jax import lax

BLOCK_EXTENT = 128
PANEL_COLUMNS = 512
SB = 128
RB = 192
WB = 64
GRP = 16
NG = 8
WG = 4
PGR = 12
SBL = 16
WLC = 8
PARENT_ROWS = 24
PARENT_COLUMNS = 4
PANEL_SUBROWS = 8
N_HALF = 2
N_ROW = 8
N_COL = 8


def spd_blocks(base_key, block_count):
    random_key, pivot_key, lead_key, side_key = jax.random.split(base_key, 4)
    shape = (block_count, PANEL_COLUMNS, PANEL_COLUMNS)
    random_part = jax.random.uniform(random_key, shape, jnp.float32, -1.0, 1.0)
    lead = jax.random.uniform(lead_key, (block_count, PANEL_COLUMNS), jnp.float32, 1.5, 2.5)
    side = jax.random.uniform(side_key, (block_count, PANEL_COLUMNS), jnp.float32, -1.5, 1.5)
    mirror = 0.5 * (random_part + jnp.swapaxes(random_part, 1, 2))
    pivots = jax.random.uniform(pivot_key, (block_count, PANEL_COLUMNS), jnp.float32, 1.2 * PANEL_COLUMNS, 2.4 * PANEL_COLUMNS)
    identity = jnp.eye(PANEL_COLUMNS, dtype=jnp.float32)
    coupling = lead[:, :, None] * lead[:, None, :] + side[:, :, None] * side[:, None, :]
    return mirror * (1.0 - identity) + identity * pivots[:, :, None] + coupling


def draw_child_diag(key, part):
    return spd_blocks(jax.random.fold_in(key, 3), 2)


def draw_parent_diag(key, part):
    return spd_blocks(jax.random.fold_in(key, 5), 1)[0]


def draw_index_maps(key, part):
    row_count = GRP // 2
    run_count = NG // row_count
    leading_count = min(WG, row_count)
    chosen = []
    for child_id in range(2):
        child_key = jax.random.fold_in(key, 11 + child_id)
        perm_key, bit_key, group_key = jax.random.split(child_key, 3)
        pick_key = jax.random.fold_in(child_key, 29)
        order_key = jax.random.fold_in(child_key, 31)
        runs = jax.vmap(lambda sub_key: jax.random.permutation(sub_key, row_count))(jax.random.split(perm_key, run_count)).astype(jnp.int32)
        leading = jax.random.permutation(pick_key, leading_count)[:2].astype(jnp.int32)
        shuffled = jax.random.permutation(order_key, row_count).astype(jnp.int32)
        keep = jnp.all(shuffled[:, None] != leading[None, :], axis=1)
        others = shuffled[jnp.nonzero(keep, size=row_count - 2)[0]]
        order = jnp.concatenate([leading, others])
        first_run = jnp.zeros((row_count,), jnp.int32).at[order].set(jnp.arange(row_count, dtype=jnp.int32))
        residues = runs.at[0].set(first_run).reshape(NG)
        half_bits = jax.random.randint(bit_key, (NG,), 0, 2)
        shifts = residues + row_count * half_bits
        shuffled_groups = jax.random.permutation(group_key, PGR - 1 - WG)
        later_groups = jnp.nonzero(shuffled_groups < NG - WG - 1, size=NG - WG - 1)[0] + WG
        targets = jnp.concatenate([jnp.arange(WG), later_groups, jnp.array([PGR - 1])])
        offsets = jnp.arange(GRP)
        blocks = GRP * targets[:, None] + (offsets[None, :] + shifts[:, None]) % GRP
        chosen.append(blocks.reshape(SB))
    return jnp.stack(chosen).astype(jnp.int32)


def shard_levels(key, dims, shards, least, high):
    def one(position, shards_of):
        steps = jax.random.uniform(jax.random.fold_in(jax.random.fold_in(key, 6), position), (shards_of,), jnp.float32, least / len(shards), high / len(shards))
        return jnp.repeat(jnp.exp(steps), dims[position] // shards_of).reshape((-1,) + (1,) * (len(dims) - position - 1))

    factor_of = one(*shards[0])
    for cut in shards[1:]:
        factor_of = factor_of * one(*cut)
    return factor_of


def centred(key, dims, spread, most, shards=(), kind=jnp.bfloat16):
    factor_of = shard_levels(key, dims, shards, -0.22, 0.18) if shards else 1.0
    values = jax.random.normal(key, dims, jnp.float32) * spread * factor_of
    return jnp.minimum(jnp.maximum(values, -most), most).astype(kind)


def setup_inputs(seed: int = 0) -> dict:
    key_of = jax.random.split(jax.random.key(seed), 7)
    child_diag = draw_child_diag(jax.random.fold_in(key_of[6], 71), 0)
    child_panel = centred(key_of[1], (2, SBL, N_ROW, BLOCK_EXTENT, PANEL_COLUMNS), 3.0, 18.0, ((0, 2), (2, 8)), jnp.float32)
    child_window = centred(key_of[2], (2, SBL, N_ROW, BLOCK_EXTENT, WLC, N_COL, BLOCK_EXTENT), 1.0, 6.0, ((0, 2), (2, 8), (5, 8)), jnp.float32)
    parent_diag = draw_parent_diag(jax.random.fold_in(key_of[6], 71), 0)
    parent_lead_panel = centred(key_of[4], (PARENT_ROWS, N_ROW, N_HALF, N_COL, PANEL_SUBROWS, PANEL_COLUMNS), 4.0, 24.0, ((1, 8), (2, 2), (3, 8)), jnp.float32)
    index_maps = draw_index_maps(jax.random.fold_in(key_of[6], 71), 0)
    return {"child_diag": child_diag, "child_panel": child_panel, "child_window": child_window, "parent_diag": parent_diag, "parent_lead_panel": parent_lead_panel, "index_maps": index_maps}


def right_solve(factor_low, row_block):
    return jax.scipy.linalg.solve_triangular(factor_low, row_block.T, lower=True).T

def reference(child_diag, child_panel, child_window, parent_diag, parent_lead_panel, index_maps):
    highest = lax.Precision.HIGHEST
    columns = WB * BLOCK_EXTENT
    pivot_lower_factor = jnp.linalg.cholesky(parent_diag)
    parent_row_blocks = right_solve(pivot_lower_factor, parent_lead_panel.reshape(RB * BLOCK_EXTENT, PANEL_COLUMNS))
    assembled_front = jnp.zeros((RB * BLOCK_EXTENT, columns), jnp.float32)
    inside = jnp.arange(BLOCK_EXTENT, dtype=jnp.int32)
    for child_id in range(2):
        child_low = jnp.linalg.cholesky(child_diag[child_id])
        child_rows = right_solve(child_low, child_panel[child_id].reshape(SB * BLOCK_EXTENT, PANEL_COLUMNS))
        schur_part = child_window[child_id].reshape(SB * BLOCK_EXTENT, columns) - jnp.dot(child_rows, child_rows[:columns].T, precision=highest)
        row_index = (index_maps[child_id][:, None] * BLOCK_EXTENT + inside[None, :]).reshape(SB * BLOCK_EXTENT).astype(jnp.int32)
        assembled_front = assembled_front.at[row_index[:, None], row_index[None, :columns]].add(schur_part)
    assembled_front = assembled_front - jnp.dot(parent_row_blocks, parent_row_blocks[:columns].T, precision=highest)
    return (assembled_front.reshape(PARENT_ROWS, N_ROW, BLOCK_EXTENT, PARENT_COLUMNS, N_HALF, N_COL, BLOCK_EXTENT), parent_row_blocks.reshape(PARENT_ROWS, N_ROW, N_HALF, N_COL, PANEL_SUBROWS, PANEL_COLUMNS), pivot_lower_factor)
```

```python
import jax
import jax.numpy as jnp
from jax import lax
from jax.sharding import PartitionSpec as P

BLOCK_EXTENT = 128
PB = 4
SB = 128
RB = 192
WB = 64


def from_root(shard, axis, root):
    mine = lax.axis_index(axis) == root
    return lax.psum(jnp.where(mine, shard, jnp.zeros_like(shard)), axis)


def pick_ranked(owners, values, wanted, slot_count, missing):
    matches = owners[..., None, :] == wanted[:, None]
    ranking = jnp.cumsum(matches.astype(jnp.int32), axis=-1) - 1
    slot_ids = jnp.arange(slot_count, dtype=jnp.int32)
    chosen = matches[..., None, :] & (ranking[..., None, :] == slot_ids[:, None])
    present = jnp.any(chosen, axis=-1)
    picked = jnp.sum(jnp.where(chosen, values[..., None, None, :], 0), axis=-1)
    return jnp.where(present, picked, missing)


def per_device(child_diag, child_panel, child_window, parent_diag, parent_lead_panel, index_maps):
    highest = lax.Precision.HIGHEST
    row_size = lax.axis_size("row")
    col_size = lax.axis_size("col")
    half_id = lax.axis_index("half")
    row_id = lax.axis_index("row")
    col_id = lax.axis_index("col")
    panel_width = PB * BLOCK_EXTENT
    group_size = 2 * row_size
    row_local = SB // row_size
    col_local = WB // row_size
    parent_row_blocks = RB // row_size
    parent_cols = WB // group_size
    per_row = 2 * (SB // group_size) // row_size
    per_col = (WB // group_size + row_size - 1) // row_size
    transpose_perm = [(i * col_size + j, j * row_size + i) for i in range(row_size) for j in range(col_size)]
    child_lead = child_panel[0, :col_local, 0]
    child_col_rows = lax.ppermute(child_lead, ("row", "col"), transpose_perm)
    sub_rows = parent_lead_panel.shape[4]
    own_rows = parent_lead_panel.reshape(-1, panel_width)
    gathered = lax.all_gather(
        parent_lead_panel.reshape(parent_row_blocks, sub_rows, panel_width),
        ("half", "col"),
        axis=1,
        tiled=True,
    )
    paired = gathered[: 2 * parent_cols].reshape(parent_cols, 2, BLOCK_EXTENT, panel_width)
    offered = lax.dynamic_index_in_dim(paired, half_id, axis=1, keepdims=False)
    parent_col_rows = lax.ppermute(offered, ("row", "col"), transpose_perm)
    eye = jnp.eye(panel_width, dtype=jnp.float32)
    child_low = jnp.linalg.cholesky(child_diag[0])
    child_inv = lax.linalg.triangular_solve(child_low, eye, left_side=True, lower=True)
    child_rows = child_panel.reshape(-1, panel_width)
    dims = (((1,), (1,)), ((), ()))
    child_factor = lax.dot_general(child_rows, child_inv, dims, precision=highest)
    child_columns = lax.dot_general(
        child_col_rows.reshape(-1, panel_width), child_inv, dims, precision=highest
    )
    schur_part = child_window.reshape(row_local * BLOCK_EXTENT, col_local * BLOCK_EXTENT) - lax.dot_general(
        child_factor, child_columns, dims, precision=highest
    )
    schur_blocks = schur_part.reshape(row_local, BLOCK_EXTENT, col_local, BLOCK_EXTENT)
    pivot_lower_factor = jnp.linalg.cholesky(parent_diag)
    parent_inv = lax.linalg.triangular_solve(pivot_lower_factor, eye, left_side=True, lower=True)
    solved = lax.dot_general(own_rows, parent_inv, dims, precision=highest)
    parent_factor = solved.reshape(parent_lead_panel.shape)
    row_factor = lax.dot_general(gathered.reshape(-1, panel_width), parent_inv, dims, precision=highest)
    column_factor = lax.dot_general(
        parent_col_rows.reshape(-1, panel_width), parent_inv, dims, precision=highest
    )
    update = lax.dot_general(row_factor, column_factor, dims, precision=highest)
    child_map = lax.dynamic_index_in_dim(index_maps, half_id, axis=0, keepdims=False)
    my_rows = lax.dynamic_index_in_dim(
        child_map.reshape(row_local, row_size), row_id, axis=1, keepdims=False
    )
    my_cols = lax.dynamic_index_in_dim(
        child_map[:WB].reshape(col_local, row_size), col_id, axis=1, keepdims=False
    )
    local_rows = jnp.arange(row_local, dtype=jnp.int32)
    local_cols = jnp.arange(col_local, dtype=jnp.int32)
    send_rows = pick_ranked(
        my_rows % row_size, local_rows, jnp.arange(row_size, dtype=jnp.int32), per_row, row_local
    )
    send_cols = pick_ranked(
        my_cols % group_size,
        local_cols,
        jnp.arange(group_size, dtype=jnp.int32),
        per_col,
        col_local,
    )
    all_rows = index_maps.reshape(2, row_local, row_size).transpose(0, 2, 1)
    row_target = pick_ranked(
        all_rows % row_size, all_rows // row_size, row_id[None], per_row, parent_row_blocks
    )[:, :, 0, :]
    all_cols = index_maps[:, :WB].reshape(2, col_local, row_size).transpose(0, 2, 1)
    col_target = pick_ranked(
        all_cols % group_size,
        all_cols // group_size,
        (half_id * row_size + col_id)[None],
        per_col,
        parent_cols,
    )[:, :, 0, :]
    assembled_front = jnp.zeros(
        (parent_row_blocks, BLOCK_EXTENT, parent_cols, BLOCK_EXTENT), jnp.float32
    )
    row_index = send_rows[None, :, None, :, None]
    col_index = send_cols.reshape(2, row_size, per_col)[:, None, :, None, :]
    outgoing = schur_blocks.at[row_index, :, col_index, :].get(mode="fill", fill_value=0.0)
    arrived = lax.all_to_all(
        outgoing.reshape(-1, per_row * per_col, BLOCK_EXTENT, BLOCK_EXTENT),
        ("half", "row", "col"),
        split_axis=0,
        concat_axis=0,
        tiled=True,
    )
    arrived = arrived.reshape(2, row_size, row_size, per_row, per_col, BLOCK_EXTENT, BLOCK_EXTENT)
    target_rows = row_target[:, :, None, :, None]
    target_cols = col_target[:, None, :, None, :]
    assembled_front = assembled_front.at[target_rows, :, target_cols, :].add(arrived, mode="drop")
    flat_front = assembled_front.reshape(
        parent_row_blocks * BLOCK_EXTENT, parent_cols * BLOCK_EXTENT
    )
    updated = flat_front - update
    return (
        updated.reshape(parent_row_blocks, 1, BLOCK_EXTENT, parent_cols, 1, 1, BLOCK_EXTENT),
        parent_factor,
        pivot_lower_factor,
    )


def solution(mesh):
    in_specs = (
        P("half", None, None),
        P("half", None, "row", None, None),
        P("half", None, "row", None, None, "col", None),
        P(),
        P(None, "row", "half", "col", None, None),
        P(),
    )
    out_specs = (
        P(None, "row", None, None, "half", "col", None),
        P(None, "row", "half", "col", None, None),
        P(),
    )
    return jax.shard_map(
        per_device, mesh=mesh, in_specs=in_specs, out_specs=out_specs, check_vma=False
    )
```

```python
import jax
import jax.numpy as jnp
from jax import lax
from jax.sharding import PartitionSpec as P

BLOCK_EXTENT = 128
PB = 4
SB = 128
RB = 192
WB = 64


def from_root(shard, axis, root):
    mine = lax.axis_index(axis) == root
    return lax.psum(jnp.where(mine, shard, jnp.zeros_like(shard)), axis)


def pick_ranked(owners, values, wanted, slot_count, missing):
    matches = owners[..., None, :] == wanted[:, None]
    ranking = jnp.cumsum(matches.astype(jnp.int32), axis=-1) - 1
    slot_ids = jnp.arange(slot_count, dtype=jnp.int32)
    chosen = matches[..., None, :] & (ranking[..., None, :] == slot_ids[:, None])
    present = jnp.any(chosen, axis=-1)
    picked = jnp.sum(jnp.where(chosen, values[..., None, None, :], 0), axis=-1)
    return jnp.where(present, picked, missing)


def _dot_t(x, y):
    return lax.dot_general(x, y, (((1,), (1,)), ((), ())), precision=lax.Precision.HIGHEST)


def _dot(x, y):
    return jnp.dot(x, y, precision=lax.Precision.HIGHEST)


def factor_and_inverse(spd, leaf):
    order = spd.shape[0]
    blocks = order // leaf
    work = spd
    columns = []
    inverses = []
    eye = jnp.eye(leaf, dtype=spd.dtype)
    for k in range(blocks):
        low = jnp.linalg.cholesky(work[:leaf, :leaf])
        inv = lax.linalg.triangular_solve(low, eye, left_side=True, lower=True)
        inverses.append(inv)
        if k < blocks - 1:
            below = _dot_t(work[leaf:, :leaf], inv)
            work = work[leaf:, leaf:] - _dot_t(below, below)
            columns.append(jnp.concatenate([low, below], axis=0))
        else:
            columns.append(low)
    lower = jnp.concatenate(
        [jnp.pad(c, ((order - c.shape[0], 0), (0, 0))) for c in columns], axis=1
    )
    size = leaf
    while len(inverses) > 1:
        merged = []
        for t in range(0, len(inverses), 2):
            start = t * size
            first, second = inverses[t], inverses[t + 1]
            coupling = lower[start + size : start + 2 * size, start : start + size]
            corner = -_dot(second, _dot(coupling, first))
            top = jnp.concatenate([first, jnp.zeros_like(first)], axis=1)
            bottom = jnp.concatenate([corner, second], axis=1)
            merged.append(jnp.concatenate([top, bottom], axis=0))
        inverses = merged
        size *= 2
    return lower, inverses[0]


def per_device(child_diag, child_panel, child_window, parent_diag, parent_lead_panel, index_maps):
    highest = lax.Precision.HIGHEST
    row_size = lax.axis_size("row")
    col_size = lax.axis_size("col")
    half_id = lax.axis_index("half")
    row_id = lax.axis_index("row")
    col_id = lax.axis_index("col")
    panel_width = PB * BLOCK_EXTENT
    group_size = 2 * row_size
    row_local = SB // row_size
    col_local = WB // row_size
    parent_row_blocks = RB // row_size
    parent_cols = WB // group_size
    per_row = 2 * (SB // group_size) // row_size
    per_col = (WB // group_size + row_size - 1) // row_size
    transpose_perm = [(i * col_size + j, j * row_size + i) for i in range(row_size) for j in range(col_size)]
    child_lead = child_panel[0, :col_local, 0]
    child_col_rows = lax.ppermute(child_lead, ("row", "col"), transpose_perm)
    sub_rows = parent_lead_panel.shape[4]
    own_rows = parent_lead_panel.reshape(-1, panel_width)
    gathered = lax.all_gather(
        parent_lead_panel.reshape(parent_row_blocks, sub_rows, panel_width),
        ("half", "col"),
        axis=1,
        tiled=True,
    )
    paired = gathered[: 2 * parent_cols].reshape(parent_cols, 2, BLOCK_EXTENT, panel_width)
    offered = lax.dynamic_index_in_dim(paired, half_id, axis=1, keepdims=False)
    parent_col_rows = lax.ppermute(offered, ("row", "col"), transpose_perm)
    child_low, child_inv = factor_and_inverse(child_diag[0], BLOCK_EXTENT)
    child_rows = child_panel.reshape(-1, panel_width)
    dims = (((1,), (1,)), ((), ()))
    child_factor = lax.dot_general(child_rows, child_inv, dims, precision=highest)
    child_columns = lax.dot_general(
        child_col_rows.reshape(-1, panel_width), child_inv, dims, precision=highest
    )
    window_blocks = child_window.reshape(row_local, BLOCK_EXTENT, col_local, BLOCK_EXTENT).transpose(0, 2, 1, 3)
    products = jnp.einsum(
        "ipk,jqk->ijpq",
        child_factor.reshape(row_local, BLOCK_EXTENT, panel_width),
        child_columns.reshape(col_local, BLOCK_EXTENT, panel_width),
        precision=highest,
    )
    schur_flat = (window_blocks - products).reshape(row_local * col_local, BLOCK_EXTENT, BLOCK_EXTENT)
    child_map = lax.dynamic_index_in_dim(index_maps, half_id, axis=0, keepdims=False)
    my_rows = lax.dynamic_index_in_dim(
        child_map.reshape(row_local, row_size), row_id, axis=1, keepdims=False
    )
    my_cols = lax.dynamic_index_in_dim(
        child_map[:WB].reshape(col_local, row_size), col_id, axis=1, keepdims=False
    )
    local_rows = jnp.arange(row_local, dtype=jnp.int32)
    local_cols = jnp.arange(col_local, dtype=jnp.int32)
    send_rows = pick_ranked(
        my_rows % row_size, local_rows, jnp.arange(row_size, dtype=jnp.int32), per_row, row_local
    )
    send_cols = pick_ranked(
        my_cols % group_size,
        local_cols,
        jnp.arange(group_size, dtype=jnp.int32),
        per_col,
        col_local,
    )
    all_rows = index_maps.reshape(2, row_local, row_size).transpose(0, 2, 1)
    row_target = pick_ranked(
        all_rows % row_size, all_rows // row_size, row_id[None], per_row, parent_row_blocks
    )[:, :, 0, :]
    all_cols = index_maps[:, :WB].reshape(2, col_local, row_size).transpose(0, 2, 1)
    col_target = pick_ranked(
        all_cols % group_size,
        all_cols // group_size,
        (half_id * row_size + col_id)[None],
        per_col,
        parent_cols,
    )[:, :, 0, :]
    block_count = row_local * col_local
    send_ok = (send_rows[None, :, None, :, None] < row_local) & (
        send_cols.reshape(2, row_size, per_col)[:, None, :, None, :] < col_local
    )
    send_index = jnp.where(
        send_ok,
        send_rows[None, :, None, :, None] * col_local
        + send_cols.reshape(2, row_size, per_col)[:, None, :, None, :],
        block_count,
    )
    padded = jnp.concatenate(
        [schur_flat, jnp.zeros((1, BLOCK_EXTENT, BLOCK_EXTENT), jnp.float32)], axis=0
    )
    outgoing = jnp.take(padded, send_index.reshape(-1), axis=0, mode="clip")
    outgoing, gathered, parent_col_rows, parent_diag = lax.optimization_barrier(
        (outgoing, gathered, parent_col_rows, parent_diag)
    )
    pivot_lower_factor, parent_inv = factor_and_inverse(parent_diag, BLOCK_EXTENT)
    solved = lax.dot_general(own_rows, parent_inv, dims, precision=highest)
    parent_factor = solved.reshape(parent_lead_panel.shape)
    row_factor = lax.dot_general(gathered.reshape(-1, panel_width), parent_inv, dims, precision=highest)
    column_factor = lax.dot_general(
        parent_col_rows.reshape(-1, panel_width), parent_inv, dims, precision=highest
    )
    update = lax.dot_general(row_factor, column_factor, dims, precision=highest)
    arrived = lax.all_to_all(
        outgoing.reshape(-1, per_row * per_col, BLOCK_EXTENT, BLOCK_EXTENT),
        ("half", "row", "col"),
        split_axis=0,
        concat_axis=0,
        tiled=True,
    )
    slot_shape = (2, row_size, row_size, per_row, per_col)
    slot_rows = jnp.broadcast_to(row_target[:, :, None, :, None], slot_shape).reshape(2, -1)
    slot_cols = jnp.broadcast_to(col_target[:, None, :, None, :], slot_shape).reshape(2, -1)
    slots = slot_rows.shape[1]
    match = (slot_rows[:, None, None, :] == jnp.arange(parent_row_blocks, dtype=jnp.int32)[None, :, None, None]) & (
        slot_cols[:, None, None, :] == jnp.arange(parent_cols, dtype=jnp.int32)[None, None, :, None]
    )
    slot_of = jnp.sum(jnp.where(match, jnp.arange(slots, dtype=jnp.int32), 0), axis=-1)
    present = jnp.any(match, axis=-1)
    slot_of = slot_of + slots * jnp.arange(2, dtype=jnp.int32)[:, None, None]
    taken = jnp.take(
        arrived.reshape(2 * slots, BLOCK_EXTENT, BLOCK_EXTENT), slot_of.reshape(-1), axis=0, mode="clip"
    ).reshape(2, parent_row_blocks, parent_cols, BLOCK_EXTENT, BLOCK_EXTENT)
    taken = jnp.where(present[..., None, None], taken, 0.0)
    assembled = (taken[0] + taken[1]).transpose(0, 2, 1, 3)
    updated = assembled - update.reshape(parent_row_blocks, BLOCK_EXTENT, parent_cols, BLOCK_EXTENT)
    return (
        updated.reshape(parent_row_blocks, 1, BLOCK_EXTENT, parent_cols, 1, 1, BLOCK_EXTENT),
        parent_factor,
        pivot_lower_factor,
    )


def solution(mesh):
    in_specs = (
        P("half", None, None),
        P("half", None, "row", None, None),
        P("half", None, "row", None, None, "col", None),
        P(),
        P(None, "row", "half", "col", None, None),
        P(),
    )
    out_specs = (
        P(None, "row", None, None, "half", "col", None),
        P(None, "row", "half", "col", None, None),
        P(),
    )
    return jax.shard_map(
        per_device, mesh=mesh, in_specs=in_specs, out_specs=out_specs, check_vma=False
    )
```

```python
import jax
import jax.numpy as jnp
from jax import lax
from jax.sharding import PartitionSpec as P

BLOCK_EXTENT = 128
PB = 4
SB = 128
RB = 192
WB = 64


def from_root(shard, axis, root):
    mine = lax.axis_index(axis) == root
    return lax.psum(jnp.where(mine, shard, jnp.zeros_like(shard)), axis)


def pick_ranked(owners, values, wanted, slot_count, missing):
    matches = owners[..., None, :] == wanted[:, None]
    ranking = jnp.cumsum(matches.astype(jnp.int32), axis=-1) - 1
    slot_ids = jnp.arange(slot_count, dtype=jnp.int32)
    chosen = matches[..., None, :] & (ranking[..., None, :] == slot_ids[:, None])
    present = jnp.any(chosen, axis=-1)
    picked = jnp.sum(jnp.where(chosen, values[..., None, None, :], 0), axis=-1)
    return jnp.where(present, picked, missing)


def _dot_t(x, y):
    return lax.dot_general(x, y, (((1,), (1,)), ((), ())), precision=lax.Precision.HIGHEST)


def _dot(x, y):
    return jnp.dot(x, y, precision=lax.Precision.HIGHEST)


def factor_and_inverse(spd, leaf):
    order = spd.shape[0]
    blocks = order // leaf
    work = spd
    columns = []
    inverses = []
    eye = jnp.eye(leaf, dtype=spd.dtype)
    for k in range(blocks):
        low = jnp.linalg.cholesky(work[:leaf, :leaf])
        inv = lax.linalg.triangular_solve(low, eye, left_side=True, lower=True)
        inverses.append(inv)
        if k < blocks - 1:
            below = _dot_t(work[leaf:, :leaf], inv)
            work = work[leaf:, leaf:] - _dot_t(below, below)
            columns.append(jnp.concatenate([low, below], axis=0))
        else:
            columns.append(low)
    lower = jnp.concatenate(
        [jnp.pad(c, ((order - c.shape[0], 0), (0, 0))) for c in columns], axis=1
    )
    size = leaf
    while len(inverses) > 1:
        merged = []
        for t in range(0, len(inverses), 2):
            start = t * size
            first, second = inverses[t], inverses[t + 1]
            coupling = lower[start + size : start + 2 * size, start : start + size]
            corner = -_dot(second, _dot(coupling, first))
            top = jnp.concatenate([first, jnp.zeros_like(first)], axis=1)
            bottom = jnp.concatenate([corner, second], axis=1)
            merged.append(jnp.concatenate([top, bottom], axis=0))
        inverses = merged
        size *= 2
    return lower, inverses[0]


def per_device(child_diag, child_panel, child_window, parent_diag, parent_lead_panel, index_maps):
    highest = lax.Precision.HIGHEST
    row_size = lax.axis_size("row")
    col_size = lax.axis_size("col")
    half_id = lax.axis_index("half")
    row_id = lax.axis_index("row")
    col_id = lax.axis_index("col")
    panel_width = PB * BLOCK_EXTENT
    group_size = 2 * row_size
    row_local = SB // row_size
    col_local = WB // row_size
    parent_row_blocks = RB // row_size
    parent_cols = WB // group_size
    per_row = 2 * (SB // group_size) // row_size
    per_col = (WB // group_size + row_size - 1) // row_size
    transpose_perm = [(i * col_size + j, j * row_size + i) for i in range(row_size) for j in range(col_size)]
    child_lead = child_panel[0, :col_local, 0]
    child_col_rows = lax.ppermute(child_lead, ("row", "col"), transpose_perm)
    sub_rows = parent_lead_panel.shape[4]
    own_rows = parent_lead_panel.reshape(-1, panel_width)
    gathered = lax.all_gather(
        parent_lead_panel.reshape(parent_row_blocks, sub_rows, panel_width),
        ("half", "col"),
        axis=1,
        tiled=True,
    )
    paired = gathered[: 2 * parent_cols].reshape(parent_cols, 2, BLOCK_EXTENT, panel_width)
    offered = lax.dynamic_index_in_dim(paired, half_id, axis=1, keepdims=False)
    parent_col_rows = lax.ppermute(offered, ("row", "col"), transpose_perm)
    child_low, child_inv = factor_and_inverse(child_diag[0], BLOCK_EXTENT)
    child_rows = child_panel.reshape(-1, panel_width)
    dims = (((1,), (1,)), ((), ()))
    child_factor = lax.dot_general(child_rows, child_inv, dims, precision=highest)
    child_columns = lax.dot_general(
        child_col_rows.reshape(-1, panel_width), child_inv, dims, precision=highest
    )
    schur_part = child_window.reshape(row_local * BLOCK_EXTENT, col_local * BLOCK_EXTENT) - lax.dot_general(
        child_factor, child_columns, dims, precision=highest
    )
    schur_blocks = schur_part.reshape(row_local, BLOCK_EXTENT, col_local, BLOCK_EXTENT)
    child_map = lax.dynamic_index_in_dim(index_maps, half_id, axis=0, keepdims=False)
    my_rows = lax.dynamic_index_in_dim(
        child_map.reshape(row_local, row_size), row_id, axis=1, keepdims=False
    )
    my_cols = lax.dynamic_index_in_dim(
        child_map[:WB].reshape(col_local, row_size), col_id, axis=1, keepdims=False
    )
    local_rows = jnp.arange(row_local, dtype=jnp.int32)
    local_cols = jnp.arange(col_local, dtype=jnp.int32)
    send_rows = pick_ranked(
        my_rows % row_size, local_rows, jnp.arange(row_size, dtype=jnp.int32), per_row, row_local
    )
    send_cols = pick_ranked(
        my_cols % group_size,
        local_cols,
        jnp.arange(group_size, dtype=jnp.int32),
        per_col,
        col_local,
    )
    all_rows = index_maps.reshape(2, row_local, row_size).transpose(0, 2, 1)
    row_target = pick_ranked(
        all_rows % row_size, all_rows // row_size, row_id[None], per_row, parent_row_blocks
    )[:, :, 0, :]
    all_cols = index_maps[:, :WB].reshape(2, col_local, row_size).transpose(0, 2, 1)
    col_target = pick_ranked(
        all_cols % group_size,
        all_cols // group_size,
        (half_id * row_size + col_id)[None],
        per_col,
        parent_cols,
    )[:, :, 0, :]
    send_row_index = jnp.minimum(send_rows, row_local - 1)[None, :, None, :, None]
    send_col_index = jnp.minimum(send_cols, col_local - 1).reshape(2, row_size, per_col)[:, None, :, None, :]
    outgoing = schur_blocks[send_row_index, :, send_col_index, :]
    outgoing, gathered, parent_col_rows, parent_diag = lax.optimization_barrier(
        (outgoing, gathered, parent_col_rows, parent_diag)
    )
    pivot_lower_factor, parent_inv = factor_and_inverse(parent_diag, BLOCK_EXTENT)
    solved = lax.dot_general(own_rows, parent_inv, dims, precision=highest)
    parent_factor = solved.reshape(parent_lead_panel.shape)
    row_factor = lax.dot_general(gathered.reshape(-1, panel_width), parent_inv, dims, precision=highest)
    column_factor = lax.dot_general(
        parent_col_rows.reshape(-1, panel_width), parent_inv, dims, precision=highest
    )
    update = lax.dot_general(row_factor, column_factor, dims, precision=highest)
    arrived = lax.all_to_all(
        outgoing.reshape(-1, per_row * per_col, BLOCK_EXTENT, BLOCK_EXTENT),
        ("half", "row", "col"),
        split_axis=0,
        concat_axis=0,
        tiled=True,
    )
    slot_shape = (2, row_size, row_size, per_row, per_col)
    slot_rows = jnp.broadcast_to(row_target[:, :, None, :, None], slot_shape).reshape(2, -1)
    slot_cols = jnp.broadcast_to(col_target[:, None, :, None, :], slot_shape).reshape(2, -1)
    slots = slot_rows.shape[1]
    match = (slot_rows[:, None, None, :] == jnp.arange(parent_row_blocks, dtype=jnp.int32)[None, :, None, None]) & (
        slot_cols[:, None, None, :] == jnp.arange(parent_cols, dtype=jnp.int32)[None, None, :, None]
    )
    slot_of = jnp.sum(jnp.where(match, jnp.arange(slots, dtype=jnp.int32), 0), axis=-1)
    present = jnp.any(match, axis=-1)
    flat_arrived = arrived.reshape(2, slots, BLOCK_EXTENT, BLOCK_EXTENT)
    first = jnp.take(flat_arrived[0], slot_of[0].reshape(-1), axis=0, mode="clip")
    second = jnp.take(flat_arrived[1], slot_of[1].reshape(-1), axis=0, mode="clip")
    block_shape = (parent_row_blocks, parent_cols, BLOCK_EXTENT, BLOCK_EXTENT)
    assembled = jnp.where(present[0, :, :, None, None], first.reshape(block_shape), 0.0) + jnp.where(
        present[1, :, :, None, None], second.reshape(block_shape), 0.0
    )
    updated = assembled.transpose(0, 2, 1, 3) - update.reshape(
        parent_row_blocks, BLOCK_EXTENT, parent_cols, BLOCK_EXTENT
    )
    return (
        updated.reshape(parent_row_blocks, 1, BLOCK_EXTENT, parent_cols, 1, 1, BLOCK_EXTENT),
        parent_factor,
        pivot_lower_factor,
    )


def solution(mesh):
    in_specs = (
        P("half", None, None),
        P("half", None, "row", None, None),
        P("half", None, "row", None, None, "col", None),
        P(),
        P(None, "row", "half", "col", None, None),
        P(),
    )
    out_specs = (
        P(None, "row", None, None, "half", "col", None),
        P(None, "row", "half", "col", None, None),
        P(),
    )
    return jax.shard_map(
        per_device, mesh=mesh, in_specs=in_specs, out_specs=out_specs, check_vma=False
    )
```

```python
import jax
import jax.numpy as jnp
from jax import lax
from jax.sharding import PartitionSpec as P
from jax.experimental import pallas as pl
from jax.experimental.pallas import tpu as pltpu

BLOCK_EXTENT = 128
PB = 4
SB = 128
RB = 192
WB = 64


def from_root(shard, axis, root):
    mine = lax.axis_index(axis) == root
    return lax.psum(jnp.where(mine, shard, jnp.zeros_like(shard)), axis)


def pick_ranked(owners, values, wanted, slot_count, missing):
    matches = owners[..., None, :] == wanted[:, None]
    ranking = jnp.cumsum(matches.astype(jnp.int32), axis=-1) - 1
    slot_ids = jnp.arange(slot_count, dtype=jnp.int32)
    chosen = matches[..., None, :] & (ranking[..., None, :] == slot_ids[:, None])
    present = jnp.any(chosen, axis=-1)
    picked = jnp.sum(jnp.where(chosen, values[..., None, None, :], 0), axis=-1)
    return jnp.where(present, picked, missing)


WAVE = 32


def _gather_blocks_kernel(row_ref, col_ref, src_ref, dst_ref, sems):
    extent = dst_ref.shape[1]
    waves = dst_ref.shape[0] // WAVE

    def one_wave(wave, carry):
        copies = []
        for t in range(WAVE):
            slot = wave * WAVE + t
            row = row_ref[slot]
            col = col_ref[slot]
            copy = pltpu.make_async_copy(
                src_ref.at[pl.ds(row * extent, extent), pl.ds(col * extent, extent)],
                dst_ref.at[slot],
                sems.at[t],
            )
            copy.start()
            copies.append(copy)
        for copy in copies:
            copy.wait()
        return carry

    lax.fori_loop(0, waves, one_wave, 0)


def gather_blocks(matrix, rows, cols, extent):
    count = rows.shape[0]
    return pl.pallas_call(
        _gather_blocks_kernel,
        out_shape=jax.ShapeDtypeStruct((count, extent, extent), matrix.dtype),
        grid_spec=pltpu.PrefetchScalarGridSpec(
            num_scalar_prefetch=2,
            grid=(1,),
            in_specs=[pl.BlockSpec(memory_space=pl.ANY)],
            out_specs=pl.BlockSpec(memory_space=pl.ANY),
            scratch_shapes=[pltpu.SemaphoreType.DMA((WAVE,))],
        ),
    )(rows, cols, matrix)


def _dot_t(x, y):
    return lax.dot_general(x, y, (((1,), (1,)), ((), ())), precision=lax.Precision.HIGHEST)


def _dot(x, y):
    return jnp.dot(x, y, precision=lax.Precision.HIGHEST)


def factor_and_inverse(spd, leaf):
    order = spd.shape[0]
    blocks = order // leaf
    work = spd
    columns = []
    inverses = []
    eye = jnp.eye(leaf, dtype=spd.dtype)
    for k in range(blocks):
        low = jnp.linalg.cholesky(work[:leaf, :leaf])
        inv = lax.linalg.triangular_solve(low, eye, left_side=True, lower=True)
        inverses.append(inv)
        if k < blocks - 1:
            below = _dot_t(work[leaf:, :leaf], inv)
            work = work[leaf:, leaf:] - _dot_t(below, below)
            columns.append(jnp.concatenate([low, below], axis=0))
        else:
            columns.append(low)
    lower = jnp.concatenate(
        [jnp.pad(c, ((order - c.shape[0], 0), (0, 0))) for c in columns], axis=1
    )
    size = leaf
    while len(inverses) > 1:
        merged = []
        for t in range(0, len(inverses), 2):
            start = t * size
            first, second = inverses[t], inverses[t + 1]
            coupling = lower[start + size : start + 2 * size, start : start + size]
            corner = -_dot(second, _dot(coupling, first))
            top = jnp.concatenate([first, jnp.zeros_like(first)], axis=1)
            bottom = jnp.concatenate([corner, second], axis=1)
            merged.append(jnp.concatenate([top, bottom], axis=0))
        inverses = merged
        size *= 2
    return lower, inverses[0]


def per_device(child_diag, child_panel, child_window, parent_diag, parent_lead_panel, index_maps):
    highest = lax.Precision.HIGHEST
    row_size = lax.axis_size("row")
    col_size = lax.axis_size("col")
    half_id = lax.axis_index("half")
    row_id = lax.axis_index("row")
    col_id = lax.axis_index("col")
    panel_width = PB * BLOCK_EXTENT
    group_size = 2 * row_size
    row_local = SB // row_size
    col_local = WB // row_size
    parent_row_blocks = RB // row_size
    parent_cols = WB // group_size
    per_row = 2 * (SB // group_size) // row_size
    per_col = (WB // group_size + row_size - 1) // row_size
    transpose_perm = [(i * col_size + j, j * row_size + i) for i in range(row_size) for j in range(col_size)]
    child_lead = child_panel[0, :col_local, 0]
    child_col_rows = lax.ppermute(child_lead, ("row", "col"), transpose_perm)
    sub_rows = parent_lead_panel.shape[4]
    own_rows = parent_lead_panel.reshape(-1, panel_width)
    gathered = lax.all_gather(
        parent_lead_panel.reshape(parent_row_blocks, sub_rows, panel_width),
        ("half", "col"),
        axis=1,
        tiled=True,
    )
    paired = gathered[: 2 * parent_cols].reshape(parent_cols, 2, BLOCK_EXTENT, panel_width)
    offered = lax.dynamic_index_in_dim(paired, half_id, axis=1, keepdims=False)
    parent_col_rows = lax.ppermute(offered, ("row", "col"), transpose_perm)
    child_low, child_inv = factor_and_inverse(child_diag[0], BLOCK_EXTENT)
    child_rows = child_panel.reshape(-1, panel_width)
    dims = (((1,), (1,)), ((), ()))
    child_factor = lax.dot_general(child_rows, child_inv, dims, precision=highest)
    child_columns = lax.dot_general(
        child_col_rows.reshape(-1, panel_width), child_inv, dims, precision=highest
    )
    schur_part = child_window.reshape(row_local * BLOCK_EXTENT, col_local * BLOCK_EXTENT) - lax.dot_general(
        child_factor, child_columns, dims, precision=highest
    )
    child_map = lax.dynamic_index_in_dim(index_maps, half_id, axis=0, keepdims=False)
    my_rows = lax.dynamic_index_in_dim(
        child_map.reshape(row_local, row_size), row_id, axis=1, keepdims=False
    )
    my_cols = lax.dynamic_index_in_dim(
        child_map[:WB].reshape(col_local, row_size), col_id, axis=1, keepdims=False
    )
    local_rows = jnp.arange(row_local, dtype=jnp.int32)
    local_cols = jnp.arange(col_local, dtype=jnp.int32)
    send_rows = pick_ranked(
        my_rows % row_size, local_rows, jnp.arange(row_size, dtype=jnp.int32), per_row, row_local
    )
    send_cols = pick_ranked(
        my_cols % group_size,
        local_cols,
        jnp.arange(group_size, dtype=jnp.int32),
        per_col,
        col_local,
    )
    all_rows = index_maps.reshape(2, row_local, row_size).transpose(0, 2, 1)
    row_target = pick_ranked(
        all_rows % row_size, all_rows // row_size, row_id[None], per_row, parent_row_blocks
    )[:, :, 0, :]
    all_cols = index_maps[:, :WB].reshape(2, col_local, row_size).transpose(0, 2, 1)
    col_target = pick_ranked(
        all_cols % group_size,
        all_cols // group_size,
        (half_id * row_size + col_id)[None],
        per_col,
        parent_cols,
    )[:, :, 0, :]
    slot_shape = (2, row_size, row_size, per_row, per_col)
    send_row_index = jnp.broadcast_to(
        jnp.minimum(send_rows, row_local - 1)[None, :, None, :, None], slot_shape
    ).reshape(-1)
    send_col_index = jnp.broadcast_to(
        jnp.minimum(send_cols, col_local - 1).reshape(2, row_size, per_col)[:, None, :, None, :],
        slot_shape,
    ).reshape(-1)
    outgoing = gather_blocks(schur_part, send_row_index, send_col_index, BLOCK_EXTENT)
    outgoing, gathered, parent_col_rows, parent_diag = lax.optimization_barrier(
        (outgoing, gathered, parent_col_rows, parent_diag)
    )
    pivot_lower_factor, parent_inv = factor_and_inverse(parent_diag, BLOCK_EXTENT)
    solved = lax.dot_general(own_rows, parent_inv, dims, precision=highest)
    parent_factor = solved.reshape(parent_lead_panel.shape)
    row_factor = lax.dot_general(gathered.reshape(-1, panel_width), parent_inv, dims, precision=highest)
    column_factor = lax.dot_general(
        parent_col_rows.reshape(-1, panel_width), parent_inv, dims, precision=highest
    )
    update = lax.dot_general(row_factor, column_factor, dims, precision=highest)
    arrived = lax.all_to_all(
        outgoing.reshape(-1, per_row * per_col, BLOCK_EXTENT, BLOCK_EXTENT),
        ("half", "row", "col"),
        split_axis=0,
        concat_axis=0,
        tiled=True,
    )
    slot_rows = jnp.broadcast_to(row_target[:, :, None, :, None], slot_shape).reshape(2, -1)
    slot_cols = jnp.broadcast_to(col_target[:, None, :, None, :], slot_shape).reshape(2, -1)
    slots = slot_rows.shape[1]
    match = (slot_rows[:, None, None, :] == jnp.arange(parent_row_blocks, dtype=jnp.int32)[None, :, None, None]) & (
        slot_cols[:, None, None, :] == jnp.arange(parent_cols, dtype=jnp.int32)[None, None, :, None]
    )
    slot_of = jnp.sum(jnp.where(match, jnp.arange(slots, dtype=jnp.int32), 0), axis=-1)
    present = jnp.any(match, axis=-1)
    flat_arrived = arrived.reshape(2 * slots, BLOCK_EXTENT, BLOCK_EXTENT)
    block_shape = (parent_row_blocks, parent_cols, BLOCK_EXTENT, BLOCK_EXTENT)
    first = jnp.take(flat_arrived, slot_of[0].reshape(-1), axis=0, mode="clip")
    second = jnp.take(flat_arrived, slot_of[1].reshape(-1) + slots, axis=0, mode="clip")
    assembled = jnp.where(present[0, :, :, None, None], first.reshape(block_shape), 0.0) + jnp.where(
        present[1, :, :, None, None], second.reshape(block_shape), 0.0
    )
    updated = assembled.transpose(0, 2, 1, 3) - update.reshape(
        parent_row_blocks, BLOCK_EXTENT, parent_cols, BLOCK_EXTENT
    )
    return (
        updated.reshape(parent_row_blocks, 1, BLOCK_EXTENT, parent_cols, 1, 1, BLOCK_EXTENT),
        parent_factor,
        pivot_lower_factor,
    )


def solution(mesh):
    in_specs = (
        P("half", None, None),
        P("half", None, "row", None, None),
        P("half", None, "row", None, None, "col", None),
        P(),
        P(None, "row", "half", "col", None, None),
        P(),
    )
    out_specs = (
        P(None, "row", None, None, "half", "col", None),
        P(None, "row", "half", "col", None, None),
        P(),
    )
    return jax.shard_map(
        per_device, mesh=mesh, in_specs=in_specs, out_specs=out_specs, check_vma=False
    )
```

```python
import jax
import jax.numpy as jnp
from jax import lax
from jax.sharding import PartitionSpec as P

BLOCK_EXTENT = 128
PB = 4
SB = 128
RB = 192
WB = 64


def from_root(shard, axis, root):
    mine = lax.axis_index(axis) == root
    return lax.psum(jnp.where(mine, shard, jnp.zeros_like(shard)), axis)


def pick_ranked(owners, values, wanted, slot_count, missing):
    matches = owners[..., None, :] == wanted[:, None]
    ranking = jnp.cumsum(matches.astype(jnp.int32), axis=-1) - 1
    slot_ids = jnp.arange(slot_count, dtype=jnp.int32)
    chosen = matches[..., None, :] & (ranking[..., None, :] == slot_ids[:, None])
    present = jnp.any(chosen, axis=-1)
    picked = jnp.sum(jnp.where(chosen, values[..., None, None, :], 0), axis=-1)
    return jnp.where(present, picked, missing)


def _dot_t(x, y):
    return lax.dot_general(x, y, (((1,), (1,)), ((), ())), precision=lax.Precision.HIGHEST)


def _dot(x, y):
    return jnp.dot(x, y, precision=lax.Precision.HIGHEST)


def factor_and_inverse(spd, leaf):
    order = spd.shape[0]
    blocks = order // leaf
    work = spd
    columns = []
    inverses = []
    eye = jnp.eye(leaf, dtype=spd.dtype)
    for k in range(blocks):
        low = jnp.linalg.cholesky(work[:leaf, :leaf])
        inv = lax.linalg.triangular_solve(low, eye, left_side=True, lower=True)
        inverses.append(inv)
        if k < blocks - 1:
            below = _dot_t(work[leaf:, :leaf], inv)
            work = work[leaf:, leaf:] - _dot_t(below, below)
            columns.append(jnp.concatenate([low, below], axis=0))
        else:
            columns.append(low)
    lower = jnp.concatenate(
        [jnp.pad(c, ((order - c.shape[0], 0), (0, 0))) for c in columns], axis=1
    )
    size = leaf
    while len(inverses) > 1:
        merged = []
        for t in range(0, len(inverses), 2):
            start = t * size
            first, second = inverses[t], inverses[t + 1]
            coupling = lower[start + size : start + 2 * size, start : start + size]
            corner = -_dot(second, _dot(coupling, first))
            top = jnp.concatenate([first, jnp.zeros_like(first)], axis=1)
            bottom = jnp.concatenate([corner, second], axis=1)
            merged.append(jnp.concatenate([top, bottom], axis=0))
        inverses = merged
        size *= 2
    return lower, inverses[0]


def per_device(child_diag, child_panel, child_window, parent_diag, parent_lead_panel, index_maps):
    highest = lax.Precision.HIGHEST
    row_size = lax.axis_size("row")
    col_size = lax.axis_size("col")
    half_id = lax.axis_index("half")
    row_id = lax.axis_index("row")
    col_id = lax.axis_index("col")
    panel_width = PB * BLOCK_EXTENT
    group_size = 2 * row_size
    row_local = SB // row_size
    col_local = WB // row_size
    parent_row_blocks = RB // row_size
    parent_cols = WB // group_size
    per_row = 2 * (SB // group_size) // row_size
    per_col = (WB // group_size + row_size - 1) // row_size
    transpose_perm = [
        (i * col_size + j, j * row_size + i) for i in range(row_size) for j in range(col_size) if i != j
    ]
    on_diagonal = row_id == col_id
    child_lead = child_panel[0, :col_local, 0]
    child_col_rows = jnp.where(
        on_diagonal, child_lead, lax.ppermute(child_lead, ("row", "col"), transpose_perm)
    )
    sub_rows = parent_lead_panel.shape[4]
    own_rows = parent_lead_panel.reshape(-1, panel_width)
    gathered = lax.all_gather(
        parent_lead_panel.reshape(parent_row_blocks, sub_rows, panel_width),
        ("half", "col"),
        axis=1,
        tiled=True,
    )
    paired = gathered[: 2 * parent_cols].reshape(parent_cols, 2, BLOCK_EXTENT, panel_width)
    offered = lax.dynamic_index_in_dim(paired, half_id, axis=1, keepdims=False)
    parent_col_rows = jnp.where(
        on_diagonal, offered, lax.ppermute(offered, ("row", "col"), transpose_perm)
    )
    child_low, child_inv = factor_and_inverse(child_diag[0], BLOCK_EXTENT)
    child_rows = child_panel.reshape(-1, panel_width)
    dims = (((1,), (1,)), ((), ()))
    child_factor = lax.dot_general(child_rows, child_inv, dims, precision=highest)
    child_columns = lax.dot_general(
        child_col_rows.reshape(-1, panel_width), child_inv, dims, precision=highest
    )
    schur_part = child_window.reshape(row_local * BLOCK_EXTENT, col_local * BLOCK_EXTENT) - lax.dot_general(
        child_factor, child_columns, dims, precision=highest
    )
    child_map = lax.dynamic_index_in_dim(index_maps, half_id, axis=0, keepdims=False)
    my_rows = lax.dynamic_index_in_dim(
        child_map.reshape(row_local, row_size), row_id, axis=1, keepdims=False
    )
    my_cols = lax.dynamic_index_in_dim(
        child_map[:WB].reshape(col_local, row_size), col_id, axis=1, keepdims=False
    )
    local_rows = jnp.arange(row_local, dtype=jnp.int32)
    local_cols = jnp.arange(col_local, dtype=jnp.int32)
    send_rows = pick_ranked(
        my_rows % row_size, local_rows, jnp.arange(row_size, dtype=jnp.int32), per_row, row_local
    )
    send_cols = pick_ranked(
        my_cols % group_size,
        local_cols,
        jnp.arange(group_size, dtype=jnp.int32),
        per_col,
        col_local,
    )
    all_rows = index_maps.reshape(2, row_local, row_size).transpose(0, 2, 1)
    row_target = pick_ranked(
        all_rows % row_size, all_rows // row_size, row_id[None], per_row, parent_row_blocks
    )[:, :, 0, :]
    all_cols = index_maps[:, :WB].reshape(2, col_local, row_size).transpose(0, 2, 1)
    col_target = pick_ranked(
        all_cols % group_size,
        all_cols // group_size,
        (half_id * row_size + col_id)[None],
        per_col,
        parent_cols,
    )[:, :, 0, :]
    schur_blocks = schur_part.reshape(row_local, BLOCK_EXTENT, col_local, BLOCK_EXTENT)
    send_row_index = jnp.minimum(send_rows, row_local - 1)[None, :, None, :, None]
    send_col_index = jnp.minimum(send_cols, col_local - 1).reshape(2, row_size, per_col)[:, None, :, None, :]
    outgoing = schur_blocks[send_row_index, :, send_col_index, :]
    outgoing, gathered, parent_col_rows, parent_diag = lax.optimization_barrier(
        (outgoing, gathered, parent_col_rows, parent_diag)
    )
    pivot_lower_factor, parent_inv = factor_and_inverse(parent_diag, BLOCK_EXTENT)
    solved = lax.dot_general(own_rows, parent_inv, dims, precision=highest)
    parent_factor = solved.reshape(parent_lead_panel.shape)
    row_factor = lax.dot_general(gathered.reshape(-1, panel_width), parent_inv, dims, precision=highest)
    column_factor = lax.dot_general(
        parent_col_rows.reshape(-1, panel_width), parent_inv, dims, precision=highest
    )
    update = lax.dot_general(row_factor, column_factor, dims, precision=highest)
    arrived = lax.all_to_all(
        outgoing.reshape(-1, per_row * per_col, BLOCK_EXTENT, BLOCK_EXTENT),
        ("half", "row", "col"),
        split_axis=0,
        concat_axis=0,
        tiled=True,
    )
    slot_shape = (2, row_size, row_size, per_row, per_col)
    slot_rows = jnp.broadcast_to(row_target[:, :, None, :, None], slot_shape).reshape(2, -1)
    slot_cols = jnp.broadcast_to(col_target[:, None, :, None, :], slot_shape).reshape(2, -1)
    slots = slot_rows.shape[1]
    match = (slot_rows[:, None, None, :] == jnp.arange(parent_row_blocks, dtype=jnp.int32)[None, :, None, None]) & (
        slot_cols[:, None, None, :] == jnp.arange(parent_cols, dtype=jnp.int32)[None, None, :, None]
    )
    slot_of = jnp.sum(jnp.where(match, jnp.arange(slots, dtype=jnp.int32), 0), axis=-1)
    present = jnp.any(match, axis=-1)
    flat_arrived = arrived.reshape(2 * slots, BLOCK_EXTENT, BLOCK_EXTENT)
    block_shape = (parent_row_blocks, parent_cols, BLOCK_EXTENT, BLOCK_EXTENT)
    first = jnp.take(flat_arrived, slot_of[0].reshape(-1), axis=0, mode="clip")
    second = jnp.take(flat_arrived, slot_of[1].reshape(-1) + slots, axis=0, mode="clip")
    assembled = jnp.where(present[0, :, :, None, None], first.reshape(block_shape), 0.0) + jnp.where(
        present[1, :, :, None, None], second.reshape(block_shape), 0.0
    )
    updated = assembled.transpose(0, 2, 1, 3) - update.reshape(
        parent_row_blocks, BLOCK_EXTENT, parent_cols, BLOCK_EXTENT
    )
    return (
        updated.reshape(parent_row_blocks, 1, BLOCK_EXTENT, parent_cols, 1, 1, BLOCK_EXTENT),
        parent_factor,
        pivot_lower_factor,
    )


def solution(mesh):
    in_specs = (
        P("half", None, None),
        P("half", None, "row", None, None),
        P("half", None, "row", None, None, "col", None),
        P(),
        P(None, "row", "half", "col", None, None),
        P(),
    )
    out_specs = (
        P(None, "row", None, None, "half", "col", None),
        P(None, "row", "half", "col", None, None),
        P(),
    )
    return jax.shard_map(
        per_device, mesh=mesh, in_specs=in_specs, out_specs=out_specs, check_vma=False
    )
```

```python
import jax
import jax.numpy as jnp
from jax import lax
from jax.sharding import PartitionSpec as P

BLOCK_EXTENT = 128
PB = 4
SB = 128
RB = 192
WB = 64


def from_root(shard, axis, root):
    mine = lax.axis_index(axis) == root
    return lax.psum(jnp.where(mine, shard, jnp.zeros_like(shard)), axis)


def pick_ranked(owners, values, wanted, slot_count, missing):
    matches = owners[..., None, :] == wanted[:, None]
    ranking = jnp.cumsum(matches.astype(jnp.int32), axis=-1) - 1
    slot_ids = jnp.arange(slot_count, dtype=jnp.int32)
    chosen = matches[..., None, :] & (ranking[..., None, :] == slot_ids[:, None])
    present = jnp.any(chosen, axis=-1)
    picked = jnp.sum(jnp.where(chosen, values[..., None, None, :], 0), axis=-1)
    return jnp.where(present, picked, missing)


def _dot_t(x, y):
    return lax.dot_general(x, y, (((1,), (1,)), ((), ())), precision=lax.Precision.HIGHEST)


def _dot(x, y):
    return jnp.dot(x, y, precision=lax.Precision.HIGHEST)


def factor_and_inverse(spd, leaf):
    order = spd.shape[0]
    blocks = order // leaf
    work = spd
    columns = []
    inverses = []
    eye = jnp.eye(leaf, dtype=spd.dtype)
    for k in range(blocks):
        low = jnp.linalg.cholesky(work[:leaf, :leaf])
        inv = lax.linalg.triangular_solve(low, eye, left_side=True, lower=True)
        inverses.append(inv)
        if k < blocks - 1:
            below = _dot_t(work[leaf:, :leaf], inv)
            work = work[leaf:, leaf:] - _dot_t(below, below)
            columns.append(jnp.concatenate([low, below], axis=0))
        else:
            columns.append(low)
    lower = jnp.concatenate(
        [jnp.pad(c, ((order - c.shape[0], 0), (0, 0))) for c in columns], axis=1
    )
    size = leaf
    while len(inverses) > 1:
        merged = []
        for t in range(0, len(inverses), 2):
            start = t * size
            first, second = inverses[t], inverses[t + 1]
            coupling = lower[start + size : start + 2 * size, start : start + size]
            corner = -_dot(second, _dot(coupling, first))
            top = jnp.concatenate([first, jnp.zeros_like(first)], axis=1)
            bottom = jnp.concatenate([corner, second], axis=1)
            merged.append(jnp.concatenate([top, bottom], axis=0))
        inverses = merged
        size *= 2
    return lower, inverses[0]


def per_device(child_diag, child_panel, child_window, parent_diag, parent_lead_panel, index_maps):
    highest = lax.Precision.HIGHEST
    row_size = lax.axis_size("row")
    col_size = lax.axis_size("col")
    half_id = lax.axis_index("half")
    row_id = lax.axis_index("row")
    col_id = lax.axis_index("col")
    panel_width = PB * BLOCK_EXTENT
    group_size = 2 * row_size
    row_local = SB // row_size
    col_local = WB // row_size
    parent_row_blocks = RB // row_size
    parent_cols = WB // group_size
    per_row = 2 * (SB // group_size) // row_size
    per_col = (WB // group_size + row_size - 1) // row_size
    transpose_perm = [
        (i * col_size + j, j * row_size + i) for i in range(row_size) for j in range(col_size) if i != j
    ]
    on_diagonal = row_id == col_id
    child_lead = child_panel[0, :col_local, 0]
    child_col_rows = jnp.where(
        on_diagonal, child_lead, lax.ppermute(child_lead, ("row", "col"), transpose_perm)
    )
    sub_rows = parent_lead_panel.shape[4]
    own_rows = parent_lead_panel.reshape(-1, panel_width)
    gathered = lax.all_gather(
        parent_lead_panel.reshape(parent_row_blocks, sub_rows, panel_width),
        ("half", "col"),
        axis=1,
        tiled=True,
    )
    paired = gathered[: 2 * parent_cols].reshape(parent_cols, 2, BLOCK_EXTENT, panel_width)
    offered = lax.dynamic_index_in_dim(paired, half_id, axis=1, keepdims=False)
    parent_col_rows = jnp.where(
        on_diagonal, offered, lax.ppermute(offered, ("row", "col"), transpose_perm)
    )
    child_low, child_inv = factor_and_inverse(child_diag[0], BLOCK_EXTENT)
    child_rows = child_panel.reshape(-1, panel_width)
    dims = (((1,), (1,)), ((), ()))
    high = lax.Precision.HIGH
    child_factor = lax.dot_general(child_rows, child_inv, dims, precision=high)
    child_columns = lax.dot_general(
        child_col_rows.reshape(-1, panel_width), child_inv, dims, precision=high
    )
    schur_part = child_window.reshape(row_local * BLOCK_EXTENT, col_local * BLOCK_EXTENT) - lax.dot_general(
        child_factor, child_columns, dims, precision=high
    )
    child_map = lax.dynamic_index_in_dim(index_maps, half_id, axis=0, keepdims=False)
    my_rows = lax.dynamic_index_in_dim(
        child_map.reshape(row_local, row_size), row_id, axis=1, keepdims=False
    )
    my_cols = lax.dynamic_index_in_dim(
        child_map[:WB].reshape(col_local, row_size), col_id, axis=1, keepdims=False
    )
    local_rows = jnp.arange(row_local, dtype=jnp.int32)
    local_cols = jnp.arange(col_local, dtype=jnp.int32)
    send_rows = pick_ranked(
        my_rows % row_size, local_rows, jnp.arange(row_size, dtype=jnp.int32), per_row, row_local
    )
    send_cols = pick_ranked(
        my_cols % group_size,
        local_cols,
        jnp.arange(group_size, dtype=jnp.int32),
        per_col,
        col_local,
    )
    all_rows = index_maps.reshape(2, row_local, row_size).transpose(0, 2, 1)
    row_target = pick_ranked(
        all_rows % row_size, all_rows // row_size, row_id[None], per_row, parent_row_blocks
    )[:, :, 0, :]
    all_cols = index_maps[:, :WB].reshape(2, col_local, row_size).transpose(0, 2, 1)
    col_target = pick_ranked(
        all_cols % group_size,
        all_cols // group_size,
        (half_id * row_size + col_id)[None],
        per_col,
        parent_cols,
    )[:, :, 0, :]
    schur_blocks = schur_part.reshape(row_local, BLOCK_EXTENT, col_local, BLOCK_EXTENT)
    send_row_index = jnp.minimum(send_rows, row_local - 1)[None, :, None, :, None]
    send_col_index = jnp.minimum(send_cols, col_local - 1).reshape(2, row_size, per_col)[:, None, :, None, :]
    outgoing = schur_blocks[send_row_index, :, send_col_index, :]
    outgoing, gathered, parent_col_rows, parent_diag = lax.optimization_barrier(
        (outgoing, gathered, parent_col_rows, parent_diag)
    )
    pivot_lower_factor, parent_inv = factor_and_inverse(parent_diag, BLOCK_EXTENT)
    solved = lax.dot_general(own_rows, parent_inv, dims, precision=highest)
    parent_factor = solved.reshape(parent_lead_panel.shape)
    row_factor = lax.dot_general(gathered.reshape(-1, panel_width), parent_inv, dims, precision=highest)
    column_factor = lax.dot_general(
        parent_col_rows.reshape(-1, panel_width), parent_inv, dims, precision=highest
    )
    update = lax.dot_general(row_factor, column_factor, dims, precision=highest)
    arrived = lax.all_to_all(
        outgoing.reshape(-1, per_row * per_col, BLOCK_EXTENT, BLOCK_EXTENT),
        ("half", "row", "col"),
        split_axis=0,
        concat_axis=0,
        tiled=True,
    )
    slot_shape = (2, row_size, row_size, per_row, per_col)
    slot_rows = jnp.broadcast_to(row_target[:, :, None, :, None], slot_shape).reshape(2, -1)
    slot_cols = jnp.broadcast_to(col_target[:, None, :, None, :], slot_shape).reshape(2, -1)
    slots = slot_rows.shape[1]
    match = (slot_rows[:, None, None, :] == jnp.arange(parent_row_blocks, dtype=jnp.int32)[None, :, None, None]) & (
        slot_cols[:, None, None, :] == jnp.arange(parent_cols, dtype=jnp.int32)[None, None, :, None]
    )
    slot_of = jnp.sum(jnp.where(match, jnp.arange(slots, dtype=jnp.int32), 0), axis=-1)
    present = jnp.any(match, axis=-1)
    flat_arrived = arrived.reshape(2 * slots, BLOCK_EXTENT, BLOCK_EXTENT)
    block_shape = (parent_row_blocks, parent_cols, BLOCK_EXTENT, BLOCK_EXTENT)
    first = jnp.take(flat_arrived, slot_of[0].reshape(-1), axis=0, mode="clip")
    second = jnp.take(flat_arrived, slot_of[1].reshape(-1) + slots, axis=0, mode="clip")
    assembled = jnp.where(present[0, :, :, None, None], first.reshape(block_shape), 0.0) + jnp.where(
        present[1, :, :, None, None], second.reshape(block_shape), 0.0
    )
    updated = assembled.transpose(0, 2, 1, 3) - update.reshape(
        parent_row_blocks, BLOCK_EXTENT, parent_cols, BLOCK_EXTENT
    )
    return (
        updated.reshape(parent_row_blocks, 1, BLOCK_EXTENT, parent_cols, 1, 1, BLOCK_EXTENT),
        parent_factor,
        pivot_lower_factor,
    )


def solution(mesh):
    in_specs = (
        P("half", None, None),
        P("half", None, "row", None, None),
        P("half", None, "row", None, None, "col", None),
        P(),
        P(None, "row", "half", "col", None, None),
        P(),
    )
    out_specs = (
        P(None, "row", None, None, "half", "col", None),
        P(None, "row", "half", "col", None, None),
        P(),
    )
    return jax.shard_map(
        per_device, mesh=mesh, in_specs=in_specs, out_specs=out_specs, check_vma=False
    )
```

```python
import jax
import jax.numpy as jnp
from jax import lax
from jax.sharding import PartitionSpec as P

BLOCK_EXTENT = 128
PB = 4
SB = 128
RB = 192
WB = 64


def from_root(shard, axis, root):
    mine = lax.axis_index(axis) == root
    return lax.psum(jnp.where(mine, shard, jnp.zeros_like(shard)), axis)


def pick_ranked(owners, values, wanted, slot_count, missing):
    matches = owners[..., None, :] == wanted[:, None]
    ranking = jnp.cumsum(matches.astype(jnp.int32), axis=-1) - 1
    slot_ids = jnp.arange(slot_count, dtype=jnp.int32)
    chosen = matches[..., None, :] & (ranking[..., None, :] == slot_ids[:, None])
    present = jnp.any(chosen, axis=-1)
    picked = jnp.sum(jnp.where(chosen, values[..., None, None, :], 0), axis=-1)
    return jnp.where(present, picked, missing)


def _dot_t(x, y):
    return lax.dot_general(x, y, (((1,), (1,)), ((), ())), precision=lax.Precision.HIGHEST)


def _dot(x, y):
    return jnp.dot(x, y, precision=lax.Precision.HIGHEST)


def factor_and_inverse(spd, leaf):
    order = spd.shape[0]
    blocks = order // leaf
    work = spd
    columns = []
    inverses = []
    eye = jnp.eye(leaf, dtype=spd.dtype)
    for k in range(blocks):
        low = jnp.linalg.cholesky(work[:leaf, :leaf])
        inv = lax.linalg.triangular_solve(low, eye, left_side=True, lower=True)
        inverses.append(inv)
        if k < blocks - 1:
            below = _dot_t(work[leaf:, :leaf], inv)
            work = work[leaf:, leaf:] - _dot_t(below, below)
            columns.append(jnp.concatenate([low, below], axis=0))
        else:
            columns.append(low)
    lower = jnp.concatenate(
        [jnp.pad(c, ((order - c.shape[0], 0), (0, 0))) for c in columns], axis=1
    )
    size = leaf
    while len(inverses) > 1:
        merged = []
        for t in range(0, len(inverses), 2):
            start = t * size
            first, second = inverses[t], inverses[t + 1]
            coupling = lower[start + size : start + 2 * size, start : start + size]
            corner = -_dot(second, _dot(coupling, first))
            top = jnp.concatenate([first, jnp.zeros_like(first)], axis=1)
            bottom = jnp.concatenate([corner, second], axis=1)
            merged.append(jnp.concatenate([top, bottom], axis=0))
        inverses = merged
        size *= 2
    return lower, inverses[0]


def per_device(child_diag, child_panel, child_window, parent_diag, parent_lead_panel, index_maps):
    highest = lax.Precision.HIGHEST
    row_size = lax.axis_size("row")
    col_size = lax.axis_size("col")
    half_id = lax.axis_index("half")
    row_id = lax.axis_index("row")
    col_id = lax.axis_index("col")
    panel_width = PB * BLOCK_EXTENT
    group_size = 2 * row_size
    row_local = SB // row_size
    col_local = WB // row_size
    parent_row_blocks = RB // row_size
    parent_cols = WB // group_size
    per_row = 2 * (SB // group_size) // row_size
    per_col = (WB // group_size + row_size - 1) // row_size
    transpose_perm = [
        (i * col_size + j, j * row_size + i) for i in range(row_size) for j in range(col_size) if i != j
    ]
    on_diagonal = row_id == col_id
    child_lead = child_panel[0, :col_local, 0]
    child_col_rows = jnp.where(
        on_diagonal, child_lead, lax.ppermute(child_lead, ("row", "col"), transpose_perm)
    )
    sub_rows = parent_lead_panel.shape[4]
    own_rows = parent_lead_panel.reshape(-1, panel_width)
    gathered = lax.all_gather(
        parent_lead_panel.reshape(parent_row_blocks, sub_rows, panel_width),
        ("half", "col"),
        axis=1,
        tiled=True,
    )
    paired = gathered[: 2 * parent_cols].reshape(parent_cols, 2, BLOCK_EXTENT, panel_width)
    offered = lax.dynamic_index_in_dim(paired, half_id, axis=1, keepdims=False)
    parent_col_rows = jnp.where(
        on_diagonal, offered, lax.ppermute(offered, ("row", "col"), transpose_perm)
    )
    child_low, child_inv = factor_and_inverse(child_diag[0], BLOCK_EXTENT)
    child_rows = child_panel.reshape(-1, panel_width)
    dims = (((1,), (1,)), ((), ()))
    high = lax.Precision.HIGH
    child_factor = lax.dot_general(child_rows, child_inv, dims, precision=high)
    child_columns = lax.dot_general(
        child_col_rows.reshape(-1, panel_width), child_inv, dims, precision=high
    )
    schur_part = child_window.reshape(row_local * BLOCK_EXTENT, col_local * BLOCK_EXTENT) - lax.dot_general(
        child_factor, child_columns, dims, precision=high
    )
    child_map = lax.dynamic_index_in_dim(index_maps, half_id, axis=0, keepdims=False)
    my_rows = lax.dynamic_index_in_dim(
        child_map.reshape(row_local, row_size), row_id, axis=1, keepdims=False
    )
    my_cols = lax.dynamic_index_in_dim(
        child_map[:WB].reshape(col_local, row_size), col_id, axis=1, keepdims=False
    )
    local_rows = jnp.arange(row_local, dtype=jnp.int32)
    local_cols = jnp.arange(col_local, dtype=jnp.int32)
    send_rows = pick_ranked(
        my_rows % row_size, local_rows, jnp.arange(row_size, dtype=jnp.int32), per_row, row_local
    )
    send_cols = pick_ranked(
        my_cols % group_size,
        local_cols,
        jnp.arange(group_size, dtype=jnp.int32),
        per_col,
        col_local,
    )
    all_rows = index_maps.reshape(2, row_local, row_size).transpose(0, 2, 1)
    row_target = pick_ranked(
        all_rows % row_size, all_rows // row_size, row_id[None], per_row, parent_row_blocks
    )[:, :, 0, :]
    all_cols = index_maps[:, :WB].reshape(2, col_local, row_size).transpose(0, 2, 1)
    col_target = pick_ranked(
        all_cols % group_size,
        all_cols // group_size,
        (half_id * row_size + col_id)[None],
        per_col,
        parent_cols,
    )[:, :, 0, :]
    schur_blocks = schur_part.reshape(row_local, BLOCK_EXTENT, col_local, BLOCK_EXTENT)
    send_row_index = jnp.minimum(send_rows, row_local - 1)[None, :, None, :, None]
    send_col_index = jnp.minimum(send_cols, col_local - 1).reshape(2, row_size, per_col)[:, None, :, None, :]
    outgoing = schur_blocks[send_row_index, :, send_col_index, :]
    outgoing, gathered, parent_diag = lax.optimization_barrier((outgoing, gathered, parent_diag))
    pivot_lower_factor, parent_inv = factor_and_inverse(parent_diag, BLOCK_EXTENT)
    solved = lax.dot_general(own_rows, parent_inv, dims, precision=highest)
    parent_factor = solved.reshape(parent_lead_panel.shape)
    row_factor = lax.dot_general(gathered.reshape(-1, panel_width), parent_inv, dims, precision=highest)
    column_factor = lax.dot_general(
        parent_col_rows.reshape(-1, panel_width), parent_inv, dims, precision=highest
    )
    update = lax.dot_general(row_factor, column_factor, dims, precision=highest)
    arrived = lax.all_to_all(
        outgoing.reshape(-1, per_row * per_col, BLOCK_EXTENT, BLOCK_EXTENT),
        ("half", "row", "col"),
        split_axis=0,
        concat_axis=0,
        tiled=True,
    )
    slot_shape = (2, row_size, row_size, per_row, per_col)
    slot_rows = jnp.broadcast_to(row_target[:, :, None, :, None], slot_shape).reshape(2, -1)
    slot_cols = jnp.broadcast_to(col_target[:, None, :, None, :], slot_shape).reshape(2, -1)
    slots = slot_rows.shape[1]
    match = (slot_rows[:, None, None, :] == jnp.arange(parent_row_blocks, dtype=jnp.int32)[None, :, None, None]) & (
        slot_cols[:, None, None, :] == jnp.arange(parent_cols, dtype=jnp.int32)[None, None, :, None]
    )
    slot_of = jnp.sum(jnp.where(match, jnp.arange(slots, dtype=jnp.int32), 0), axis=-1)
    present = jnp.any(match, axis=-1)
    flat_arrived = arrived.reshape(2 * slots, BLOCK_EXTENT, BLOCK_EXTENT)
    block_shape = (parent_row_blocks, parent_cols, BLOCK_EXTENT, BLOCK_EXTENT)
    first = jnp.take(flat_arrived, slot_of[0].reshape(-1), axis=0, mode="clip")
    second = jnp.take(flat_arrived, slot_of[1].reshape(-1) + slots, axis=0, mode="clip")
    assembled = jnp.where(present[0, :, :, None, None], first.reshape(block_shape), 0.0) + jnp.where(
        present[1, :, :, None, None], second.reshape(block_shape), 0.0
    )
    updated = assembled.transpose(0, 2, 1, 3) - update.reshape(
        parent_row_blocks, BLOCK_EXTENT, parent_cols, BLOCK_EXTENT
    )
    return (
        updated.reshape(parent_row_blocks, 1, BLOCK_EXTENT, parent_cols, 1, 1, BLOCK_EXTENT),
        parent_factor,
        pivot_lower_factor,
    )


def solution(mesh):
    in_specs = (
        P("half", None, None),
        P("half", None, "row", None, None),
        P("half", None, "row", None, None, "col", None),
        P(),
        P(None, "row", "half", "col", None, None),
        P(),
    )
    out_specs = (
        P(None, "row", None, None, "half", "col", None),
        P(None, "row", "half", "col", None, None),
        P(),
    )
    return jax.shard_map(
        per_device, mesh=mesh, in_specs=in_specs, out_specs=out_specs, check_vma=False
    )
```

```python
import jax
import jax.numpy as jnp
from jax import lax
from jax.sharding import PartitionSpec as P

BLOCK_EXTENT = 128
PB = 4
SB = 128
RB = 192
WB = 64


def from_root(shard, axis, root):
    mine = lax.axis_index(axis) == root
    return lax.psum(jnp.where(mine, shard, jnp.zeros_like(shard)), axis)


def pick_ranked(owners, values, wanted, slot_count, missing):
    matches = owners[..., None, :] == wanted[:, None]
    ranking = jnp.cumsum(matches.astype(jnp.int32), axis=-1) - 1
    slot_ids = jnp.arange(slot_count, dtype=jnp.int32)
    chosen = matches[..., None, :] & (ranking[..., None, :] == slot_ids[:, None])
    present = jnp.any(chosen, axis=-1)
    picked = jnp.sum(jnp.where(chosen, values[..., None, None, :], 0), axis=-1)
    return jnp.where(present, picked, missing)


def _dot_t(x, y):
    return lax.dot_general(x, y, (((1,), (1,)), ((), ())), precision=lax.Precision.HIGHEST)


def _dot(x, y):
    return jnp.dot(x, y, precision=lax.Precision.HIGHEST)


def factor_and_inverse(spd, leaf):
    order = spd.shape[0]
    blocks = order // leaf
    work = spd
    columns = []
    inverses = []
    eye = jnp.eye(leaf, dtype=spd.dtype)
    for k in range(blocks):
        low = jnp.linalg.cholesky(work[:leaf, :leaf])
        inv = lax.linalg.triangular_solve(low, eye, left_side=True, lower=True)
        inverses.append(inv)
        if k < blocks - 1:
            below = _dot_t(work[leaf:, :leaf], inv)
            work = work[leaf:, leaf:] - _dot_t(below, below)
            columns.append(jnp.concatenate([low, below], axis=0))
        else:
            columns.append(low)
    lower = jnp.concatenate(
        [jnp.pad(c, ((order - c.shape[0], 0), (0, 0))) for c in columns], axis=1
    )
    size = leaf
    while len(inverses) > 1:
        merged = []
        for t in range(0, len(inverses), 2):
            start = t * size
            first, second = inverses[t], inverses[t + 1]
            coupling = lower[start + size : start + 2 * size, start : start + size]
            corner = -_dot(second, _dot(coupling, first))
            top = jnp.concatenate([first, jnp.zeros_like(first)], axis=1)
            bottom = jnp.concatenate([corner, second], axis=1)
            merged.append(jnp.concatenate([top, bottom], axis=0))
        inverses = merged
        size *= 2
    return lower, inverses[0]


def per_device(child_diag, child_panel, child_window, parent_diag, parent_lead_panel, index_maps):
    highest = lax.Precision.HIGHEST
    row_size = lax.axis_size("row")
    col_size = lax.axis_size("col")
    half_id = lax.axis_index("half")
    row_id = lax.axis_index("row")
    col_id = lax.axis_index("col")
    panel_width = PB * BLOCK_EXTENT
    group_size = 2 * row_size
    row_local = SB // row_size
    col_local = WB // row_size
    parent_row_blocks = RB // row_size
    parent_cols = WB // group_size
    per_row = 2 * (SB // group_size) // row_size
    per_col = (WB // group_size + row_size - 1) // row_size
    transpose_perm = [
        (i * col_size + j, j * row_size + i) for i in range(row_size) for j in range(col_size) if i != j
    ]
    on_diagonal = row_id == col_id
    child_lead = child_panel[0, :col_local, 0]
    child_col_rows = jnp.where(
        on_diagonal, child_lead, lax.ppermute(child_lead, ("row", "col"), transpose_perm)
    )
    sub_rows = parent_lead_panel.shape[4]
    own_rows = parent_lead_panel.reshape(-1, panel_width)
    gathered = lax.all_gather(
        parent_lead_panel.reshape(parent_row_blocks, sub_rows, panel_width),
        ("half", "col"),
        axis=1,
        tiled=True,
    )
    child_low, child_inv = factor_and_inverse(child_diag[0], BLOCK_EXTENT)
    child_rows = child_panel.reshape(-1, panel_width)
    dims = (((1,), (1,)), ((), ()))
    high = lax.Precision.HIGH
    child_factor = lax.dot_general(child_rows, child_inv, dims, precision=high)
    child_columns = lax.dot_general(
        child_col_rows.reshape(-1, panel_width), child_inv, dims, precision=high
    )
    schur_part = child_window.reshape(row_local * BLOCK_EXTENT, col_local * BLOCK_EXTENT) - lax.dot_general(
        child_factor, child_columns, dims, precision=high
    )
    gathered_late, schur_part = lax.optimization_barrier((gathered, schur_part))
    paired = gathered_late[: 2 * parent_cols].reshape(parent_cols, 2, BLOCK_EXTENT, panel_width)
    offered = lax.dynamic_index_in_dim(paired, half_id, axis=1, keepdims=False)
    parent_col_rows = jnp.where(
        on_diagonal, offered, lax.ppermute(offered, ("row", "col"), transpose_perm)
    )
    child_map = lax.dynamic_index_in_dim(index_maps, half_id, axis=0, keepdims=False)
    my_rows = lax.dynamic_index_in_dim(
        child_map.reshape(row_local, row_size), row_id, axis=1, keepdims=False
    )
    my_cols = lax.dynamic_index_in_dim(
        child_map[:WB].reshape(col_local, row_size), col_id, axis=1, keepdims=False
    )
    local_rows = jnp.arange(row_local, dtype=jnp.int32)
    local_cols = jnp.arange(col_local, dtype=jnp.int32)
    send_rows = pick_ranked(
        my_rows % row_size, local_rows, jnp.arange(row_size, dtype=jnp.int32), per_row, row_local
    )
    send_cols = pick_ranked(
        my_cols % group_size,
        local_cols,
        jnp.arange(group_size, dtype=jnp.int32),
        per_col,
        col_local,
    )
    all_rows = index_maps.reshape(2, row_local, row_size).transpose(0, 2, 1)
    row_target = pick_ranked(
        all_rows % row_size, all_rows // row_size, row_id[None], per_row, parent_row_blocks
    )[:, :, 0, :]
    all_cols = index_maps[:, :WB].reshape(2, col_local, row_size).transpose(0, 2, 1)
    col_target = pick_ranked(
        all_cols % group_size,
        all_cols // group_size,
        (half_id * row_size + col_id)[None],
        per_col,
        parent_cols,
    )[:, :, 0, :]
    schur_blocks = schur_part.reshape(row_local, BLOCK_EXTENT, col_local, BLOCK_EXTENT)
    send_row_index = jnp.minimum(send_rows, row_local - 1)[None, :, None, :, None]
    send_col_index = jnp.minimum(send_cols, col_local - 1).reshape(2, row_size, per_col)[:, None, :, None, :]
    outgoing = schur_blocks[send_row_index, :, send_col_index, :]
    outgoing, gathered, parent_col_rows, parent_diag = lax.optimization_barrier(
        (outgoing, gathered, parent_col_rows, parent_diag)
    )
    pivot_lower_factor, parent_inv = factor_and_inverse(parent_diag, BLOCK_EXTENT)
    solved = lax.dot_general(own_rows, parent_inv, dims, precision=highest)
    parent_factor = solved.reshape(parent_lead_panel.shape)
    row_factor = lax.dot_general(gathered.reshape(-1, panel_width), parent_inv, dims, precision=highest)
    column_factor = lax.dot_general(
        parent_col_rows.reshape(-1, panel_width), parent_inv, dims, precision=highest
    )
    update = lax.dot_general(row_factor, column_factor, dims, precision=highest)
    arrived = lax.all_to_all(
        outgoing.reshape(-1, per_row * per_col, BLOCK_EXTENT, BLOCK_EXTENT),
        ("half", "row", "col"),
        split_axis=0,
        concat_axis=0,
        tiled=True,
    )
    slot_shape = (2, row_size, row_size, per_row, per_col)
    slot_rows = jnp.broadcast_to(row_target[:, :, None, :, None], slot_shape).reshape(2, -1)
    slot_cols = jnp.broadcast_to(col_target[:, None, :, None, :], slot_shape).reshape(2, -1)
    slots = slot_rows.shape[1]
    match = (slot_rows[:, None, None, :] == jnp.arange(parent_row_blocks, dtype=jnp.int32)[None, :, None, None]) & (
        slot_cols[:, None, None, :] == jnp.arange(parent_cols, dtype=jnp.int32)[None, None, :, None]
    )
    slot_of = jnp.sum(jnp.where(match, jnp.arange(slots, dtype=jnp.int32), 0), axis=-1)
    present = jnp.any(match, axis=-1)
    flat_arrived = arrived.reshape(2 * slots, BLOCK_EXTENT, BLOCK_EXTENT)
    block_shape = (parent_row_blocks, parent_cols, BLOCK_EXTENT, BLOCK_EXTENT)
    first = jnp.take(flat_arrived, slot_of[0].reshape(-1), axis=0, mode="clip")
    second = jnp.take(flat_arrived, slot_of[1].reshape(-1) + slots, axis=0, mode="clip")
    assembled = jnp.where(present[0, :, :, None, None], first.reshape(block_shape), 0.0) + jnp.where(
        present[1, :, :, None, None], second.reshape(block_shape), 0.0
    )
    updated = assembled.transpose(0, 2, 1, 3) - update.reshape(
        parent_row_blocks, BLOCK_EXTENT, parent_cols, BLOCK_EXTENT
    )
    return (
        updated.reshape(parent_row_blocks, 1, BLOCK_EXTENT, parent_cols, 1, 1, BLOCK_EXTENT),
        parent_factor,
        pivot_lower_factor,
    )


def solution(mesh):
    in_specs = (
        P("half", None, None),
        P("half", None, "row", None, None),
        P("half", None, "row", None, None, "col", None),
        P(),
        P(None, "row", "half", "col", None, None),
        P(),
    )
    out_specs = (
        P(None, "row", None, None, "half", "col", None),
        P(None, "row", "half", "col", None, None),
        P(),
    )
    return jax.shard_map(
        per_device, mesh=mesh, in_specs=in_specs, out_specs=out_specs, check_vma=False
    )
```

```python
import jax
import jax.numpy as jnp
from jax import lax
from jax.sharding import PartitionSpec as P

BLOCK_EXTENT = 128
PB = 4
SB = 128
RB = 192
WB = 64


def from_root(shard, axis, root):
    mine = lax.axis_index(axis) == root
    return lax.psum(jnp.where(mine, shard, jnp.zeros_like(shard)), axis)


def pick_ranked(owners, values, wanted, slot_count, missing):
    matches = owners[..., None, :] == wanted[:, None]
    ranking = jnp.cumsum(matches.astype(jnp.int32), axis=-1) - 1
    slot_ids = jnp.arange(slot_count, dtype=jnp.int32)
    chosen = matches[..., None, :] & (ranking[..., None, :] == slot_ids[:, None])
    present = jnp.any(chosen, axis=-1)
    picked = jnp.sum(jnp.where(chosen, values[..., None, None, :], 0), axis=-1)
    return jnp.where(present, picked, missing)


def _dot_t(x, y):
    return lax.dot_general(x, y, (((1,), (1,)), ((), ())), precision=lax.Precision.HIGHEST)


def _dot(x, y):
    return jnp.dot(x, y, precision=lax.Precision.HIGHEST)


def factor_and_inverse(spd, leaf):
    order = spd.shape[0]
    blocks = order // leaf
    work = spd
    columns = []
    inverses = []
    eye = jnp.eye(leaf, dtype=spd.dtype)
    for k in range(blocks):
        low = jnp.linalg.cholesky(work[:leaf, :leaf])
        inv = lax.linalg.triangular_solve(low, eye, left_side=True, lower=True)
        inverses.append(inv)
        if k < blocks - 1:
            below = _dot_t(work[leaf:, :leaf], inv)
            work = work[leaf:, leaf:] - _dot_t(below, below)
            columns.append(jnp.concatenate([low, below], axis=0))
        else:
            columns.append(low)
    lower = jnp.concatenate(
        [jnp.pad(c, ((order - c.shape[0], 0), (0, 0))) for c in columns], axis=1
    )
    size = leaf
    while len(inverses) > 1:
        merged = []
        for t in range(0, len(inverses), 2):
            start = t * size
            first, second = inverses[t], inverses[t + 1]
            coupling = lower[start + size : start + 2 * size, start : start + size]
            corner = -_dot(second, _dot(coupling, first))
            top = jnp.concatenate([first, jnp.zeros_like(first)], axis=1)
            bottom = jnp.concatenate([corner, second], axis=1)
            merged.append(jnp.concatenate([top, bottom], axis=0))
        inverses = merged
        size *= 2
    return lower, inverses[0]


def per_device(child_diag, child_panel, child_window, parent_diag, parent_lead_panel, index_maps):
    highest = lax.Precision.HIGHEST
    row_size = lax.axis_size("row")
    col_size = lax.axis_size("col")
    half_id = lax.axis_index("half")
    row_id = lax.axis_index("row")
    col_id = lax.axis_index("col")
    panel_width = PB * BLOCK_EXTENT
    group_size = 2 * row_size
    row_local = SB // row_size
    col_local = WB // row_size
    parent_row_blocks = RB // row_size
    parent_cols = WB // group_size
    per_row = 2 * (SB // group_size) // row_size
    per_col = (WB // group_size + row_size - 1) // row_size
    transpose_perm = [
        (i * col_size + j, j * row_size + i) for i in range(row_size) for j in range(col_size) if i != j
    ]
    on_diagonal = row_id == col_id
    child_lead = child_panel[0, :col_local, 0]
    child_col_rows = jnp.where(
        on_diagonal, child_lead, lax.ppermute(child_lead, ("row", "col"), transpose_perm)
    )
    sub_rows = parent_lead_panel.shape[4]
    own_rows = parent_lead_panel.reshape(-1, panel_width)
    gathered = lax.all_gather(
        parent_lead_panel.reshape(parent_row_blocks, sub_rows, panel_width),
        ("half", "col"),
        axis=1,
        tiled=True,
    )
    leading_parent = parent_lead_panel.reshape(parent_row_blocks, sub_rows, panel_width)[: 2 * parent_cols]
    transposed = jnp.where(
        on_diagonal, leading_parent, lax.ppermute(leading_parent, ("row", "col"), transpose_perm)
    )
    column_blocks = lax.all_gather(transposed, ("half", "row"), axis=1, tiled=True)
    parent_col_rows = lax.dynamic_index_in_dim(
        column_blocks.reshape(parent_cols, 2, BLOCK_EXTENT, panel_width), half_id, axis=1, keepdims=False
    )
    child_low, child_inv = factor_and_inverse(child_diag[0], BLOCK_EXTENT)
    child_rows = child_panel.reshape(-1, panel_width)
    dims = (((1,), (1,)), ((), ()))
    high = lax.Precision.HIGH
    child_factor = lax.dot_general(child_rows, child_inv, dims, precision=high)
    child_columns = lax.dot_general(
        child_col_rows.reshape(-1, panel_width), child_inv, dims, precision=high
    )
    schur_part = child_window.reshape(row_local * BLOCK_EXTENT, col_local * BLOCK_EXTENT) - lax.dot_general(
        child_factor, child_columns, dims, precision=high
    )
    child_map = lax.dynamic_index_in_dim(index_maps, half_id, axis=0, keepdims=False)
    my_rows = lax.dynamic_index_in_dim(
        child_map.reshape(row_local, row_size), row_id, axis=1, keepdims=False
    )
    my_cols = lax.dynamic_index_in_dim(
        child_map[:WB].reshape(col_local, row_size), col_id, axis=1, keepdims=False
    )
    local_rows = jnp.arange(row_local, dtype=jnp.int32)
    local_cols = jnp.arange(col_local, dtype=jnp.int32)
    send_rows = pick_ranked(
        my_rows % row_size, local_rows, jnp.arange(row_size, dtype=jnp.int32), per_row, row_local
    )
    send_cols = pick_ranked(
        my_cols % group_size,
        local_cols,
        jnp.arange(group_size, dtype=jnp.int32),
        per_col,
        col_local,
    )
    all_rows = index_maps.reshape(2, row_local, row_size).transpose(0, 2, 1)
    row_target = pick_ranked(
        all_rows % row_size, all_rows // row_size, row_id[None], per_row, parent_row_blocks
    )[:, :, 0, :]
    all_cols = index_maps[:, :WB].reshape(2, col_local, row_size).transpose(0, 2, 1)
    col_target = pick_ranked(
        all_cols % group_size,
        all_cols // group_size,
        (half_id * row_size + col_id)[None],
        per_col,
        parent_cols,
    )[:, :, 0, :]
    schur_blocks = schur_part.reshape(row_local, BLOCK_EXTENT, col_local, BLOCK_EXTENT)
    send_row_index = jnp.minimum(send_rows, row_local - 1)[None, :, None, :, None]
    send_col_index = jnp.minimum(send_cols, col_local - 1).reshape(2, row_size, per_col)[:, None, :, None, :]
    outgoing = schur_blocks[send_row_index, :, send_col_index, :]
    outgoing, gathered, parent_col_rows, parent_diag = lax.optimization_barrier(
        (outgoing, gathered, parent_col_rows, parent_diag)
    )
    pivot_lower_factor, parent_inv = factor_and_inverse(parent_diag, BLOCK_EXTENT)
    solved = lax.dot_general(own_rows, parent_inv, dims, precision=highest)
    parent_factor = solved.reshape(parent_lead_panel.shape)
    row_factor = lax.dot_general(gathered.reshape(-1, panel_width), parent_inv, dims, precision=highest)
    column_factor = lax.dot_general(
        parent_col_rows.reshape(-1, panel_width), parent_inv, dims, precision=highest
    )
    update = lax.dot_general(row_factor, column_factor, dims, precision=highest)
    arrived = lax.all_to_all(
        outgoing.reshape(-1, per_row * per_col, BLOCK_EXTENT, BLOCK_EXTENT),
        ("half", "row", "col"),
        split_axis=0,
        concat_axis=0,
        tiled=True,
    )
    slot_shape = (2, row_size, row_size, per_row, per_col)
    slot_rows = jnp.broadcast_to(row_target[:, :, None, :, None], slot_shape).reshape(2, -1)
    slot_cols = jnp.broadcast_to(col_target[:, None, :, None, :], slot_shape).reshape(2, -1)
    slots = slot_rows.shape[1]
    match = (slot_rows[:, None, None, :] == jnp.arange(parent_row_blocks, dtype=jnp.int32)[None, :, None, None]) & (
        slot_cols[:, None, None, :] == jnp.arange(parent_cols, dtype=jnp.int32)[None, None, :, None]
    )
    slot_of = jnp.sum(jnp.where(match, jnp.arange(slots, dtype=jnp.int32), 0), axis=-1)
    present = jnp.any(match, axis=-1)
    flat_arrived = arrived.reshape(2 * slots, BLOCK_EXTENT, BLOCK_EXTENT)
    block_shape = (parent_row_blocks, parent_cols, BLOCK_EXTENT, BLOCK_EXTENT)
    first = jnp.take(flat_arrived, slot_of[0].reshape(-1), axis=0, mode="clip")
    second = jnp.take(flat_arrived, slot_of[1].reshape(-1) + slots, axis=0, mode="clip")
    assembled = jnp.where(present[0, :, :, None, None], first.reshape(block_shape), 0.0) + jnp.where(
        present[1, :, :, None, None], second.reshape(block_shape), 0.0
    )
    updated = assembled.transpose(0, 2, 1, 3) - update.reshape(
        parent_row_blocks, BLOCK_EXTENT, parent_cols, BLOCK_EXTENT
    )
    return (
        updated.reshape(parent_row_blocks, 1, BLOCK_EXTENT, parent_cols, 1, 1, BLOCK_EXTENT),
        parent_factor,
        pivot_lower_factor,
    )


def solution(mesh):
    in_specs = (
        P("half", None, None),
        P("half", None, "row", None, None),
        P("half", None, "row", None, None, "col", None),
        P(),
        P(None, "row", "half", "col", None, None),
        P(),
    )
    out_specs = (
        P(None, "row", None, None, "half", "col", None),
        P(None, "row", "half", "col", None, None),
        P(),
    )
    return jax.shard_map(
        per_device, mesh=mesh, in_specs=in_specs, out_specs=out_specs, check_vma=False
    )
```

```python
import jax
import jax.numpy as jnp
from jax import lax
from jax.sharding import PartitionSpec as P

BLOCK_EXTENT = 128
PB = 4
SB = 128
RB = 192
WB = 64


def from_root(shard, axis, root):
    mine = lax.axis_index(axis) == root
    return lax.psum(jnp.where(mine, shard, jnp.zeros_like(shard)), axis)


def pick_ranked(owners, values, wanted, slot_count, missing):
    matches = owners[..., None, :] == wanted[:, None]
    ranking = jnp.cumsum(matches.astype(jnp.int32), axis=-1) - 1
    slot_ids = jnp.arange(slot_count, dtype=jnp.int32)
    chosen = matches[..., None, :] & (ranking[..., None, :] == slot_ids[:, None])
    present = jnp.any(chosen, axis=-1)
    picked = jnp.sum(jnp.where(chosen, values[..., None, None, :], 0), axis=-1)
    return jnp.where(present, picked, missing)


def _dot_t(x, y):
    return lax.dot_general(x, y, (((1,), (1,)), ((), ())), precision=lax.Precision.HIGHEST)


def _dot(x, y):
    return jnp.dot(x, y, precision=lax.Precision.HIGHEST)


def factor_and_inverse(spd, leaf):
    order = spd.shape[0]
    blocks = order // leaf
    work = spd
    columns = []
    inverses = []
    eye = jnp.eye(leaf, dtype=spd.dtype)
    for k in range(blocks):
        low = jnp.linalg.cholesky(work[:leaf, :leaf])
        inv = lax.linalg.triangular_solve(low, eye, left_side=True, lower=True)
        inverses.append(inv)
        if k < blocks - 1:
            below = _dot_t(work[leaf:, :leaf], inv)
            work = work[leaf:, leaf:] - _dot_t(below, below)
            columns.append(jnp.concatenate([low, below], axis=0))
        else:
            columns.append(low)
    lower = jnp.concatenate(
        [jnp.pad(c, ((order - c.shape[0], 0), (0, 0))) for c in columns], axis=1
    )
    size = leaf
    while len(inverses) > 1:
        merged = []
        for t in range(0, len(inverses), 2):
            start = t * size
            first, second = inverses[t], inverses[t + 1]
            coupling = lower[start + size : start + 2 * size, start : start + size]
            corner = -_dot(second, _dot(coupling, first))
            top = jnp.concatenate([first, jnp.zeros_like(first)], axis=1)
            bottom = jnp.concatenate([corner, second], axis=1)
            merged.append(jnp.concatenate([top, bottom], axis=0))
        inverses = merged
        size *= 2
    return lower, inverses[0]


def per_device(child_diag, child_panel, child_window, parent_diag, parent_lead_panel, index_maps):
    highest = lax.Precision.HIGHEST
    row_size = lax.axis_size("row")
    col_size = lax.axis_size("col")
    half_id = lax.axis_index("half")
    row_id = lax.axis_index("row")
    col_id = lax.axis_index("col")
    panel_width = PB * BLOCK_EXTENT
    group_size = 2 * row_size
    row_local = SB // row_size
    col_local = WB // row_size
    parent_row_blocks = RB // row_size
    parent_cols = WB // group_size
    per_row = 2 * (SB // group_size) // row_size
    per_col = (WB // group_size + row_size - 1) // row_size
    transpose_perm = [
        (i * col_size + j, j * row_size + i) for i in range(row_size) for j in range(col_size) if i != j
    ]
    on_diagonal = row_id == col_id
    child_lead = child_panel[0, :col_local, 0]
    child_col_rows = jnp.where(
        on_diagonal, child_lead, lax.ppermute(child_lead, ("row", "col"), transpose_perm)
    )
    sub_rows = parent_lead_panel.shape[4]
    own_rows = parent_lead_panel.reshape(-1, panel_width)
    gathered = lax.all_gather(
        parent_lead_panel.reshape(parent_row_blocks, sub_rows, panel_width),
        ("half", "col"),
        axis=1,
        tiled=True,
    )
    leading_parent = parent_lead_panel.reshape(parent_row_blocks, sub_rows, panel_width)[: 2 * parent_cols]
    transposed = jnp.where(
        on_diagonal, leading_parent, lax.ppermute(leading_parent, ("row", "col"), transpose_perm)
    )
    column_blocks = lax.all_gather(transposed, ("half", "row"), axis=1, tiled=True)
    parent_col_rows = lax.dynamic_index_in_dim(
        column_blocks.reshape(parent_cols, 2, BLOCK_EXTENT, panel_width), half_id, axis=1, keepdims=False
    )
    child_low, child_inv = factor_and_inverse(child_diag[0], BLOCK_EXTENT)
    child_rows = child_panel.reshape(-1, panel_width)
    dims = (((1,), (1,)), ((), ()))
    high = lax.Precision.HIGH
    child_factor = lax.dot_general(child_rows, child_inv, dims, precision=high)
    child_columns = lax.dot_general(
        child_col_rows.reshape(-1, panel_width), child_inv, dims, precision=high
    )
    schur_part = child_window.reshape(row_local * BLOCK_EXTENT, col_local * BLOCK_EXTENT) - lax.dot_general(
        child_factor, child_columns, dims, precision=high
    )
    child_map = lax.dynamic_index_in_dim(index_maps, half_id, axis=0, keepdims=False)
    my_rows = lax.dynamic_index_in_dim(
        child_map.reshape(row_local, row_size), row_id, axis=1, keepdims=False
    )
    my_cols = lax.dynamic_index_in_dim(
        child_map[:WB].reshape(col_local, row_size), col_id, axis=1, keepdims=False
    )
    local_rows = jnp.arange(row_local, dtype=jnp.int32)
    local_cols = jnp.arange(col_local, dtype=jnp.int32)
    send_rows = pick_ranked(
        my_rows % row_size, local_rows, jnp.arange(row_size, dtype=jnp.int32), per_row, row_local
    )
    send_cols = pick_ranked(
        my_cols % group_size,
        local_cols,
        jnp.arange(group_size, dtype=jnp.int32),
        per_col,
        col_local,
    )
    all_rows = index_maps.reshape(2, row_local, row_size).transpose(0, 2, 1)
    row_target = pick_ranked(
        all_rows % row_size, all_rows // row_size, row_id[None], per_row, parent_row_blocks
    )[:, :, 0, :]
    all_cols = index_maps[:, :WB].reshape(2, col_local, row_size).transpose(0, 2, 1)
    col_target = pick_ranked(
        all_cols % group_size,
        all_cols // group_size,
        (half_id * row_size + col_id)[None],
        per_col,
        parent_cols,
    )[:, :, 0, :]
    schur_blocks = schur_part.reshape(row_local, BLOCK_EXTENT, col_local, BLOCK_EXTENT)
    send_row_index = jnp.minimum(send_rows, row_local - 1)[None, :, None, :, None]
    send_col_index = jnp.minimum(send_cols, col_local - 1).reshape(2, row_size, per_col)[:, None, :, None, :]
    outgoing = schur_blocks[send_row_index, :, send_col_index, :]
    outgoing, gathered, parent_col_rows, parent_diag = lax.optimization_barrier(
        (outgoing, gathered, parent_col_rows, parent_diag)
    )
    pivot_lower_factor, parent_inv = factor_and_inverse(parent_diag, BLOCK_EXTENT)
    solved = lax.dot_general(own_rows, parent_inv, dims, precision=highest)
    parent_factor = solved.reshape(parent_lead_panel.shape)
    row_factor = lax.dot_general(gathered.reshape(-1, panel_width), parent_inv, dims, precision=highest)
    column_factor = lax.dot_general(
        parent_col_rows.reshape(-1, panel_width), parent_inv, dims, precision=highest
    )
    update = lax.dot_general(row_factor, column_factor, dims, precision=highest)
    arrived = lax.all_to_all(
        outgoing.reshape(-1, per_row * per_col, BLOCK_EXTENT, BLOCK_EXTENT),
        ("half", "row", "col"),
        split_axis=0,
        concat_axis=0,
        tiled=True,
    )
    slot_shape = (2, row_size, row_size, per_row, per_col)
    slot_rows = jnp.broadcast_to(row_target[:, :, None, :, None], slot_shape).reshape(2, -1)
    slot_cols = jnp.broadcast_to(col_target[:, None, :, None, :], slot_shape).reshape(2, -1)
    slots = slot_rows.shape[1]
    match = (slot_rows[:, None, None, :] == jnp.arange(parent_row_blocks, dtype=jnp.int32)[None, :, None, None]) & (
        slot_cols[:, None, None, :] == jnp.arange(parent_cols, dtype=jnp.int32)[None, None, :, None]
    )
    slot_of = jnp.sum(jnp.where(match, jnp.arange(slots, dtype=jnp.int32), 0), axis=-1)
    present = jnp.any(match, axis=-1)
    rows_arrived = arrived.reshape(2 * slots * BLOCK_EXTENT, BLOCK_EXTENT)
    inside = jnp.arange(BLOCK_EXTENT, dtype=jnp.int32)[None, :, None]
    first_rows = slot_of[0][:, None, :] * BLOCK_EXTENT + inside
    second_rows = (slot_of[1][:, None, :] + slots) * BLOCK_EXTENT + inside
    out_shape = (parent_row_blocks, BLOCK_EXTENT, parent_cols, BLOCK_EXTENT)
    first = jnp.take(rows_arrived, first_rows.reshape(-1), axis=0, mode="clip").reshape(out_shape)
    second = jnp.take(rows_arrived, second_rows.reshape(-1), axis=0, mode="clip").reshape(out_shape)
    updated = (
        jnp.where(present[0][:, None, :, None], first, 0.0)
        + jnp.where(present[1][:, None, :, None], second, 0.0)
        - update.reshape(out_shape)
    )
    return (
        updated.reshape(parent_row_blocks, 1, BLOCK_EXTENT, parent_cols, 1, 1, BLOCK_EXTENT),
        parent_factor,
        pivot_lower_factor,
    )


def solution(mesh):
    in_specs = (
        P("half", None, None),
        P("half", None, "row", None, None),
        P("half", None, "row", None, None, "col", None),
        P(),
        P(None, "row", "half", "col", None, None),
        P(),
    )
    out_specs = (
        P(None, "row", None, None, "half", "col", None),
        P(None, "row", "half", "col", None, None),
        P(),
    )
    return jax.shard_map(
        per_device, mesh=mesh, in_specs=in_specs, out_specs=out_specs, check_vma=False
    )
```

```python
import jax
import jax.numpy as jnp
from jax import lax
from jax.sharding import PartitionSpec as P

BLOCK_EXTENT = 128
PB = 4
SB = 128
RB = 192
WB = 64


def from_root(shard, axis, root):
    mine = lax.axis_index(axis) == root
    return lax.psum(jnp.where(mine, shard, jnp.zeros_like(shard)), axis)


def pick_ranked(owners, values, wanted, slot_count, missing):
    matches = owners[..., None, :] == wanted[:, None]
    ranking = jnp.cumsum(matches.astype(jnp.int32), axis=-1) - 1
    slot_ids = jnp.arange(slot_count, dtype=jnp.int32)
    chosen = matches[..., None, :] & (ranking[..., None, :] == slot_ids[:, None])
    present = jnp.any(chosen, axis=-1)
    picked = jnp.sum(jnp.where(chosen, values[..., None, None, :], 0), axis=-1)
    return jnp.where(present, picked, missing)


def _dot_t(x, y):
    return lax.dot_general(x, y, (((1,), (1,)), ((), ())), precision=lax.Precision.HIGHEST)


def _dot(x, y):
    return jnp.dot(x, y, precision=lax.Precision.HIGHEST)


def factor_and_inverse(spd, leaf):
    order = spd.shape[0]
    blocks = order // leaf
    work = spd
    columns = []
    inverses = []
    eye = jnp.eye(leaf, dtype=spd.dtype)
    for k in range(blocks):
        low = jnp.linalg.cholesky(work[:leaf, :leaf])
        inv = lax.linalg.triangular_solve(low, eye, left_side=True, lower=True)
        inverses.append(inv)
        if k < blocks - 1:
            below = _dot_t(work[leaf:, :leaf], inv)
            work = work[leaf:, leaf:] - _dot_t(below, below)
            columns.append(jnp.concatenate([low, below], axis=0))
        else:
            columns.append(low)
    lower = jnp.concatenate(
        [jnp.pad(c, ((order - c.shape[0], 0), (0, 0))) for c in columns], axis=1
    )
    size = leaf
    while len(inverses) > 1:
        merged = []
        for t in range(0, len(inverses), 2):
            start = t * size
            first, second = inverses[t], inverses[t + 1]
            coupling = lower[start + size : start + 2 * size, start : start + size]
            corner = -_dot(second, _dot(coupling, first))
            top = jnp.concatenate([first, jnp.zeros_like(first)], axis=1)
            bottom = jnp.concatenate([corner, second], axis=1)
            merged.append(jnp.concatenate([top, bottom], axis=0))
        inverses = merged
        size *= 2
    return lower, inverses[0]


def per_device(child_diag, child_panel, child_window, parent_diag, parent_lead_panel, index_maps):
    highest = lax.Precision.HIGHEST
    row_size = lax.axis_size("row")
    col_size = lax.axis_size("col")
    half_id = lax.axis_index("half")
    row_id = lax.axis_index("row")
    col_id = lax.axis_index("col")
    panel_width = PB * BLOCK_EXTENT
    group_size = 2 * row_size
    row_local = SB // row_size
    col_local = WB // row_size
    parent_row_blocks = RB // row_size
    parent_cols = WB // group_size
    per_row = 2 * (SB // group_size) // row_size
    per_col = (WB // group_size + row_size - 1) // row_size
    transpose_perm = [
        (i * col_size + j, j * row_size + i) for i in range(row_size) for j in range(col_size) if i != j
    ]
    on_diagonal = row_id == col_id
    child_lead = child_panel[0, :col_local, 0]
    child_col_rows = jnp.where(
        on_diagonal, child_lead, lax.ppermute(child_lead, ("row", "col"), transpose_perm)
    )
    sub_rows = parent_lead_panel.shape[4]
    own_rows = parent_lead_panel.reshape(-1, panel_width)
    gathered = lax.all_gather(
        parent_lead_panel.reshape(parent_row_blocks, sub_rows, panel_width),
        ("half", "col"),
        axis=1,
        tiled=True,
    )
    child_low, child_inv = factor_and_inverse(child_diag[0], BLOCK_EXTENT)
    child_rows = child_panel.reshape(-1, panel_width)
    dims = (((1,), (1,)), ((), ()))
    high = lax.Precision.HIGH
    child_factor = lax.dot_general(child_rows, child_inv, dims, precision=high)
    child_columns = lax.dot_general(
        child_col_rows.reshape(-1, panel_width), child_inv, dims, precision=high
    )
    schur_part = child_window.reshape(row_local * BLOCK_EXTENT, col_local * BLOCK_EXTENT) - lax.dot_general(
        child_factor, child_columns, dims, precision=high
    )
    leading_parent = parent_lead_panel.reshape(parent_row_blocks, sub_rows, panel_width)[: 2 * parent_cols]
    leading_parent, schur_part = lax.optimization_barrier((leading_parent, schur_part))
    transposed = jnp.where(
        on_diagonal, leading_parent, lax.ppermute(leading_parent, ("row", "col"), transpose_perm)
    )
    column_blocks = lax.all_gather(transposed, ("half", "row"), axis=1, tiled=True)
    parent_col_rows = lax.dynamic_index_in_dim(
        column_blocks.reshape(parent_cols, 2, BLOCK_EXTENT, panel_width), half_id, axis=1, keepdims=False
    )
    child_map = lax.dynamic_index_in_dim(index_maps, half_id, axis=0, keepdims=False)
    my_rows = lax.dynamic_index_in_dim(
        child_map.reshape(row_local, row_size), row_id, axis=1, keepdims=False
    )
    my_cols = lax.dynamic_index_in_dim(
        child_map[:WB].reshape(col_local, row_size), col_id, axis=1, keepdims=False
    )
    local_rows = jnp.arange(row_local, dtype=jnp.int32)
    local_cols = jnp.arange(col_local, dtype=jnp.int32)
    send_rows = pick_ranked(
        my_rows % row_size, local_rows, jnp.arange(row_size, dtype=jnp.int32), per_row, row_local
    )
    send_cols = pick_ranked(
        my_cols % group_size,
        local_cols,
        jnp.arange(group_size, dtype=jnp.int32),
        per_col,
        col_local,
    )
    all_rows = index_maps.reshape(2, row_local, row_size).transpose(0, 2, 1)
    row_target = pick_ranked(
        all_rows % row_size, all_rows // row_size, row_id[None], per_row, parent_row_blocks
    )[:, :, 0, :]
    all_cols = index_maps[:, :WB].reshape(2, col_local, row_size).transpose(0, 2, 1)
    col_target = pick_ranked(
        all_cols % group_size,
        all_cols // group_size,
        (half_id * row_size + col_id)[None],
        per_col,
        parent_cols,
    )[:, :, 0, :]
    schur_blocks = schur_part.reshape(row_local, BLOCK_EXTENT, col_local, BLOCK_EXTENT)
    send_row_index = jnp.minimum(send_rows, row_local - 1)[None, :, None, :, None]
    send_col_index = jnp.minimum(send_cols, col_local - 1).reshape(2, row_size, per_col)[:, None, :, None, :]
    outgoing = schur_blocks[send_row_index, :, send_col_index, :]
    outgoing, gathered, parent_col_rows, parent_diag = lax.optimization_barrier(
        (outgoing, gathered, parent_col_rows, parent_diag)
    )
    pivot_lower_factor, parent_inv = factor_and_inverse(parent_diag, BLOCK_EXTENT)
    solved = lax.dot_general(own_rows, parent_inv, dims, precision=highest)
    parent_factor = solved.reshape(parent_lead_panel.shape)
    row_factor = lax.dot_general(gathered.reshape(-1, panel_width), parent_inv, dims, precision=highest)
    column_factor = lax.dot_general(
        parent_col_rows.reshape(-1, panel_width), parent_inv, dims, precision=highest
    )
    update = lax.dot_general(row_factor, column_factor, dims, precision=highest)
    arrived = lax.all_to_all(
        outgoing.reshape(-1, per_row * per_col, BLOCK_EXTENT, BLOCK_EXTENT),
        ("half", "row", "col"),
        split_axis=0,
        concat_axis=0,
        tiled=True,
    )
    slot_shape = (2, row_size, row_size, per_row, per_col)
    slot_rows = jnp.broadcast_to(row_target[:, :, None, :, None], slot_shape).reshape(2, -1)
    slot_cols = jnp.broadcast_to(col_target[:, None, :, None, :], slot_shape).reshape(2, -1)
    slots = slot_rows.shape[1]
    match = (slot_rows[:, None, None, :] == jnp.arange(parent_row_blocks, dtype=jnp.int32)[None, :, None, None]) & (
        slot_cols[:, None, None, :] == jnp.arange(parent_cols, dtype=jnp.int32)[None, None, :, None]
    )
    slot_of = jnp.sum(jnp.where(match, jnp.arange(slots, dtype=jnp.int32), 0), axis=-1)
    present = jnp.any(match, axis=-1)
    flat_arrived = arrived.reshape(2 * slots, BLOCK_EXTENT, BLOCK_EXTENT)
    block_shape = (parent_row_blocks, parent_cols, BLOCK_EXTENT, BLOCK_EXTENT)
    first = jnp.take(flat_arrived, slot_of[0].reshape(-1), axis=0, mode="clip")
    second = jnp.take(flat_arrived, slot_of[1].reshape(-1) + slots, axis=0, mode="clip")
    assembled = jnp.where(present[0, :, :, None, None], first.reshape(block_shape), 0.0) + jnp.where(
        present[1, :, :, None, None], second.reshape(block_shape), 0.0
    )
    updated = assembled.transpose(0, 2, 1, 3) - update.reshape(
        parent_row_blocks, BLOCK_EXTENT, parent_cols, BLOCK_EXTENT
    )
    return (
        updated.reshape(parent_row_blocks, 1, BLOCK_EXTENT, parent_cols, 1, 1, BLOCK_EXTENT),
        parent_factor,
        pivot_lower_factor,
    )


def solution(mesh):
    in_specs = (
        P("half", None, None),
        P("half", None, "row", None, None),
        P("half", None, "row", None, None, "col", None),
        P(),
        P(None, "row", "half", "col", None, None),
        P(),
    )
    out_specs = (
        P(None, "row", None, None, "half", "col", None),
        P(None, "row", "half", "col", None, None),
        P(),
    )
    return jax.shard_map(
        per_device, mesh=mesh, in_specs=in_specs, out_specs=out_specs, check_vma=False
    )
```

```python
import jax
import jax.numpy as jnp
from jax import lax
from jax.sharding import PartitionSpec as P

BLOCK_EXTENT = 128
PB = 4
SB = 128
RB = 192
WB = 64


def from_root(shard, axis, root):
    mine = lax.axis_index(axis) == root
    return lax.psum(jnp.where(mine, shard, jnp.zeros_like(shard)), axis)


def pick_ranked(owners, values, wanted, slot_count, missing):
    matches = owners[..., None, :] == wanted[:, None]
    ranking = jnp.cumsum(matches.astype(jnp.int32), axis=-1) - 1
    slot_ids = jnp.arange(slot_count, dtype=jnp.int32)
    chosen = matches[..., None, :] & (ranking[..., None, :] == slot_ids[:, None])
    present = jnp.any(chosen, axis=-1)
    picked = jnp.sum(jnp.where(chosen, values[..., None, None, :], 0), axis=-1)
    return jnp.where(present, picked, missing)


def _dot_t(x, y):
    return lax.dot_general(x, y, (((1,), (1,)), ((), ())), precision=lax.Precision.HIGHEST)


def _dot(x, y):
    return jnp.dot(x, y, precision=lax.Precision.HIGHEST)


def factor_and_inverse(spd, leaf):
    order = spd.shape[0]
    blocks = order // leaf
    work = spd
    columns = []
    inverses = []
    eye = jnp.eye(leaf, dtype=spd.dtype)
    for k in range(blocks):
        low = jnp.linalg.cholesky(work[:leaf, :leaf])
        inv = lax.linalg.triangular_solve(low, eye, left_side=True, lower=True)
        inverses.append(inv)
        if k < blocks - 1:
            below = _dot_t(work[leaf:, :leaf], inv)
            work = work[leaf:, leaf:] - _dot_t(below, below)
            columns.append(jnp.concatenate([low, below], axis=0))
        else:
            columns.append(low)
    lower = jnp.concatenate(
        [jnp.pad(c, ((order - c.shape[0], 0), (0, 0))) for c in columns], axis=1
    )
    size = leaf
    while len(inverses) > 1:
        merged = []
        for t in range(0, len(inverses), 2):
            start = t * size
            first, second = inverses[t], inverses[t + 1]
            coupling = lower[start + size : start + 2 * size, start : start + size]
            corner = -_dot(second, _dot(coupling, first))
            top = jnp.concatenate([first, jnp.zeros_like(first)], axis=1)
            bottom = jnp.concatenate([corner, second], axis=1)
            merged.append(jnp.concatenate([top, bottom], axis=0))
        inverses = merged
        size *= 2
    return lower, inverses[0]


def per_device(child_diag, child_panel, child_window, parent_diag, parent_lead_panel, index_maps):
    highest = lax.Precision.HIGHEST
    row_size = lax.axis_size("row")
    col_size = lax.axis_size("col")
    half_id = lax.axis_index("half")
    row_id = lax.axis_index("row")
    col_id = lax.axis_index("col")
    panel_width = PB * BLOCK_EXTENT
    group_size = 2 * row_size
    row_local = SB // row_size
    col_local = WB // row_size
    parent_row_blocks = RB // row_size
    parent_cols = WB // group_size
    per_row = 2 * (SB // group_size) // row_size
    per_col = (WB // group_size + row_size - 1) // row_size
    transpose_perm = [
        (i * col_size + j, j * row_size + i) for i in range(row_size) for j in range(col_size) if i != j
    ]
    on_diagonal = row_id == col_id
    child_lead = child_panel[0, :col_local, 0]
    whole_panel = child_panel[0, :, 0]
    child_col_rows = jnp.where(
        on_diagonal, whole_panel, lax.ppermute(whole_panel, ("row", "col"), transpose_perm)
    )[:col_local]
    sub_rows = parent_lead_panel.shape[4]
    own_rows = parent_lead_panel.reshape(-1, panel_width)
    gathered = lax.all_gather(
        parent_lead_panel.reshape(parent_row_blocks, sub_rows, panel_width),
        ("half", "col"),
        axis=1,
        tiled=True,
    )
    leading_parent = parent_lead_panel.reshape(parent_row_blocks, sub_rows, panel_width)[: 2 * parent_cols]
    transposed = jnp.where(
        on_diagonal, leading_parent, lax.ppermute(leading_parent, ("row", "col"), transpose_perm)
    )
    column_blocks = lax.all_gather(transposed, ("half", "row"), axis=1, tiled=True)
    parent_col_rows = lax.dynamic_index_in_dim(
        column_blocks.reshape(parent_cols, 2, BLOCK_EXTENT, panel_width), half_id, axis=1, keepdims=False
    )
    child_low, child_inv = factor_and_inverse(child_diag[0], BLOCK_EXTENT)
    child_rows = child_panel.reshape(-1, panel_width)
    dims = (((1,), (1,)), ((), ()))
    high = lax.Precision.HIGH
    child_factor = lax.dot_general(child_rows, child_inv, dims, precision=high)
    child_columns = lax.dot_general(
        child_col_rows.reshape(-1, panel_width), child_inv, dims, precision=high
    )
    schur_part = child_window.reshape(row_local * BLOCK_EXTENT, col_local * BLOCK_EXTENT) - lax.dot_general(
        child_factor, child_columns, dims, precision=high
    )
    child_map = lax.dynamic_index_in_dim(index_maps, half_id, axis=0, keepdims=False)
    my_rows = lax.dynamic_index_in_dim(
        child_map.reshape(row_local, row_size), row_id, axis=1, keepdims=False
    )
    my_cols = lax.dynamic_index_in_dim(
        child_map[:WB].reshape(col_local, row_size), col_id, axis=1, keepdims=False
    )
    local_rows = jnp.arange(row_local, dtype=jnp.int32)
    local_cols = jnp.arange(col_local, dtype=jnp.int32)
    send_rows = pick_ranked(
        my_rows % row_size, local_rows, jnp.arange(row_size, dtype=jnp.int32), per_row, row_local
    )
    send_cols = pick_ranked(
        my_cols % group_size,
        local_cols,
        jnp.arange(group_size, dtype=jnp.int32),
        per_col,
        col_local,
    )
    all_rows = index_maps.reshape(2, row_local, row_size).transpose(0, 2, 1)
    row_target = pick_ranked(
        all_rows % row_size, all_rows // row_size, row_id[None], per_row, parent_row_blocks
    )[:, :, 0, :]
    all_cols = index_maps[:, :WB].reshape(2, col_local, row_size).transpose(0, 2, 1)
    col_target = pick_ranked(
        all_cols % group_size,
        all_cols // group_size,
        (half_id * row_size + col_id)[None],
        per_col,
        parent_cols,
    )[:, :, 0, :]
    schur_blocks = schur_part.reshape(row_local, BLOCK_EXTENT, col_local, BLOCK_EXTENT)
    send_row_index = jnp.minimum(send_rows, row_local - 1)[None, :, None, :, None]
    send_col_index = jnp.minimum(send_cols, col_local - 1).reshape(2, row_size, per_col)[:, None, :, None, :]
    outgoing = schur_blocks[send_row_index, :, send_col_index, :]
    outgoing, gathered, parent_col_rows, parent_diag = lax.optimization_barrier(
        (outgoing, gathered, parent_col_rows, parent_diag)
    )
    pivot_lower_factor, parent_inv = factor_and_inverse(parent_diag, BLOCK_EXTENT)
    solved = lax.dot_general(own_rows, parent_inv, dims, precision=highest)
    parent_factor = solved.reshape(parent_lead_panel.shape)
    row_factor = lax.dot_general(gathered.reshape(-1, panel_width), parent_inv, dims, precision=highest)
    column_factor = lax.dot_general(
        parent_col_rows.reshape(-1, panel_width), parent_inv, dims, precision=highest
    )
    update = lax.dot_general(row_factor, column_factor, dims, precision=highest)
    arrived = lax.all_to_all(
        outgoing.reshape(-1, per_row * per_col, BLOCK_EXTENT, BLOCK_EXTENT),
        ("half", "row", "col"),
        split_axis=0,
        concat_axis=0,
        tiled=True,
    )
    slot_shape = (2, row_size, row_size, per_row, per_col)
    slot_rows = jnp.broadcast_to(row_target[:, :, None, :, None], slot_shape).reshape(2, -1)
    slot_cols = jnp.broadcast_to(col_target[:, None, :, None, :], slot_shape).reshape(2, -1)
    slots = slot_rows.shape[1]
    match = (slot_rows[:, None, None, :] == jnp.arange(parent_row_blocks, dtype=jnp.int32)[None, :, None, None]) & (
        slot_cols[:, None, None, :] == jnp.arange(parent_cols, dtype=jnp.int32)[None, None, :, None]
    )
    slot_of = jnp.sum(jnp.where(match, jnp.arange(slots, dtype=jnp.int32), 0), axis=-1)
    present = jnp.any(match, axis=-1)
    flat_arrived = arrived.reshape(2 * slots, BLOCK_EXTENT, BLOCK_EXTENT)
    block_shape = (parent_row_blocks, parent_cols, BLOCK_EXTENT, BLOCK_EXTENT)
    first = jnp.take(flat_arrived, slot_of[0].reshape(-1), axis=0, mode="clip")
    second = jnp.take(flat_arrived, slot_of[1].reshape(-1) + slots, axis=0, mode="clip")
    assembled = jnp.where(present[0, :, :, None, None], first.reshape(block_shape), 0.0) + jnp.where(
        present[1, :, :, None, None], second.reshape(block_shape), 0.0
    )
    updated = assembled.transpose(0, 2, 1, 3) - update.reshape(
        parent_row_blocks, BLOCK_EXTENT, parent_cols, BLOCK_EXTENT
    )
    return (
        updated.reshape(parent_row_blocks, 1, BLOCK_EXTENT, parent_cols, 1, 1, BLOCK_EXTENT),
        parent_factor,
        pivot_lower_factor,
    )


def solution(mesh):
    in_specs = (
        P("half", None, None),
        P("half", None, "row", None, None),
        P("half", None, "row", None, None, "col", None),
        P(),
        P(None, "row", "half", "col", None, None),
        P(),
    )
    out_specs = (
        P(None, "row", None, None, "half", "col", None),
        P(None, "row", "half", "col", None, None),
        P(),
    )
    return jax.shard_map(
        per_device, mesh=mesh, in_specs=in_specs, out_specs=out_specs, check_vma=False
    )
```
